32 devices in a mesh: tile: 8 (over y, x, core), dir: 4 (over z).
Axes of the slice: x: 2, y: 2, z: 4, core: 2. Of those that a mesh axis runs over, the one named last changes fastest.
Arguments:
- screens: bfloat16 [6, 512, 2048], P(None, 'tile'), may hold values from -13 to 13
- ray_shift: int32 [16, 6, 2], P('dir'), may hold values from -128 to 2047, as said below
- ray_weight: float32 [16, 6, 4], P('dir'), may hold values from 0 to 0.5
- influence_index: int32 [512, 16, 16], P('tile', 'dir'), may hold values from 0 to 69, as said below
- influence: bfloat16 [512, 16, 16, 128], P('tile', 'dir'), may hold values from 0 to 0.22
- pupil_mask: int32 [512, 2048], P('tile', 'dir'), may hold values 0 or 1
- petal: int32 [24, 48], P('tile', 'dir'), may hold values from 0 to 6
Outputs:
- commands: float32 [24, 48], P('tile', 'dir')
- corrected: bfloat16 [16, 512, 2048], P('dir', 'tile')
The draws below stay inside these ranges and needn't reach their ends.
Inputs may be any that keep to these rules, and one draw needn't show every extreme that they name: ray_shift[..., 0], the row offset, lies in -128 to 127 and reaches both ends; ray_shift[..., 1], the column offset, lies in 0 to 2047. `influence_index`: each entry names a grid point of the tile's own actuator block extended by one actuator on each side, flattened row by row with 14 points a row; entries may repeat.
All inputs are finite; a program needn't handle non-finite values. No bound on the sum of `pupil_mask` on one device may be relied on, other than what follows from the above.
Results may differ from the reference program's by a relative error of at most 0.007.
Values may be sent and summed in bfloat16 or wider, within the bound.
No kernel may reach another device: no remote copies, remote signals or barrier semaphores. Data moves between devices by JAX's collectives and lax.ppermute only.
A program may use at most 128 MiB of HBM per device.

```python
import math
import jax
import jax.numpy as jnp
from jax import lax

COLS = 2048
ROWS_DEV = 64
LAYERS = 6
SPAN = 2
AR_DEV = 3
AC_DEV = 12
NEAR = 16
ITERS = 3
PUPIL = 512
COLS_DEV = 512
DIRS = 16
AROWS = 24
ACOLS = 48


wave_count = 8


bump_width = 0.8


influence_scale = 0.12


far_level = 0.08


def draw_screens(key, part):
    wave_key, phase_key, rough_key = jax.random.split(jax.random.fold_in(key, 37), 3)
    row_wave = jax.random.randint(jax.random.fold_in(wave_key, 1), (LAYERS, wave_count), -(AROWS // 5), AROWS // 5 + 1)
    column_wave = jax.random.randint(jax.random.fold_in(wave_key, 2), (LAYERS, wave_count), 1, ACOLS // 5 + 1)
    offsets = jax.random.uniform(phase_key, (LAYERS, wave_count), jnp.float32, 0.0, 2.0 * math.pi)
    row_index = jnp.arange(PUPIL, dtype=jnp.int32)[:, None]
    column_index = jnp.arange(COLS, dtype=jnp.int32)[None, :]
    period = PUPIL * COLS
    rough = jnp.clip(jax.random.normal(rough_key, (LAYERS, PUPIL, COLS), jnp.float32), -4.0, 4.0)
    layer_list = []
    for layer_index in range(LAYERS):
        smooth = jnp.zeros((PUPIL, COLS), jnp.float32)
        for wave_index in range(wave_count):
            phase_count = jnp.mod(row_wave[layer_index, wave_index] * row_index * COLS + column_wave[layer_index, wave_index] * column_index * PUPIL, period)
            smooth = smooth + jnp.cos(phase_count.astype(jnp.float32) * (2.0 * math.pi / period) + offsets[layer_index, wave_index])
        layer_list.append(smooth)
    return (jnp.stack(layer_list) + rough).astype(jnp.bfloat16)


def draw_ray_shift(key, part):
    first_key, second_key, third_key = jax.random.split(jax.random.fold_in(key, 11), 3)
    rim_depth = SPAN * ROWS_DEV
    row_shift = jax.random.randint(first_key, (DIRS, LAYERS), -rim_depth, rim_depth)
    column_shift = jax.random.randint(second_key, (DIRS, LAYERS), 0, COLS)
    chosen = jax.random.randint(third_key, (), 0, DIRS)
    row_shift = row_shift.at[chosen, LAYERS - 1].set(rim_depth - 1)
    row_shift = row_shift.at[(chosen + 1) % DIRS, LAYERS - 1].set(-rim_depth)
    column_shift = column_shift.at[chosen, 0].set(COLS - 1)
    return jnp.stack([row_shift, column_shift], axis=-1).astype(jnp.int32)


def index_table(key):
    first_key, second_key = jax.random.split(jax.random.fold_in(key, 23), 2)
    tile_count = COLS_DEV // 128
    band_row = jnp.arange(PUPIL, dtype=jnp.int32) % ROWS_DEV
    column_tile = jnp.arange(COLS // 128, dtype=jnp.int32) % tile_count
    base_row = jnp.minimum((2 * band_row * AR_DEV + ROWS_DEV) // (2 * ROWS_DEV), AR_DEV)
    base_column = jnp.minimum((2 * column_tile * 128 * AC_DEV + COLS_DEV) // (2 * COLS_DEV), AC_DEV - 6)
    row_step = jax.random.randint(first_key, (PUPIL, COLS // 128, NEAR), 0, 2)
    column_step = jax.random.randint(second_key, (PUPIL, COLS // 128, NEAR), 0, 8)
    grid_row = base_row[:, None, None] + row_step
    grid_column = base_column[None, :, None] + column_step
    entry = jnp.arange(NEAR, dtype=jnp.int32)[None, None, :]
    first_row = (band_row == 0)[:, None, None]
    last_row = (band_row == ROWS_DEV - 1)[:, None, None]
    first_tile = (column_tile == 0)[None, :, None]
    last_tile = (column_tile == tile_count - 1)[None, :, None]
    row_entry = (entry == 0) | (entry == 3)
    grid_row = jnp.where(row_entry & first_row, 0, grid_row)
    grid_row = jnp.where(row_entry & last_row, AR_DEV + 1, grid_row)
    grid_column = jnp.where((entry == 2) & first_tile, 0, grid_column)
    grid_column = jnp.where(((entry == 1) | (entry == 3)) & last_tile, AC_DEV + 1, grid_column)
    corner_low = (entry == 4) & first_row & first_tile
    grid_row = jnp.where(corner_low, 0, grid_row)
    grid_column = jnp.where(corner_low, 0, grid_column)
    corner_right = (entry == 5) & first_row & last_tile
    grid_row = jnp.where(corner_right, 0, grid_row)
    grid_column = jnp.where(corner_right, AC_DEV + 1, grid_column)
    corner_left = (entry == 6) & last_row & first_tile
    grid_row = jnp.where(corner_left, AR_DEV + 1, grid_row)
    grid_column = jnp.where(corner_left, 0, grid_column)
    flat_index = grid_row * (AC_DEV + 2) + grid_column
    return flat_index.astype(jnp.int32)


def draw_influence_index(key, part):
    return index_table(key)


def draw_influence(key, part):
    flat_index = index_table(key)
    tile_count = COLS_DEV // 128
    band_row = (jnp.arange(PUPIL, dtype=jnp.int32) % ROWS_DEV).astype(jnp.float32)
    row_coord = (band_row + 0.5) * (AR_DEV / ROWS_DEV) - 0.5
    column_tile = jnp.arange(COLS // 128, dtype=jnp.int32) % tile_count
    pixel_column = column_tile[:, None] * 128 + jnp.arange(128, dtype=jnp.int32)[None, :]
    column_coord = (pixel_column.astype(jnp.float32) + 0.5) * (AC_DEV / COLS_DEV) - 0.5
    actuator_row = (flat_index // (AC_DEV + 2) - 1).astype(jnp.float32)
    actuator_column = (flat_index % (AC_DEV + 2) - 1).astype(jnp.float32)
    row_gap = row_coord[:, None, None, None] - actuator_row[:, :, :, None]
    column_gap = column_coord[None, :, None, :] - actuator_column[:, :, :, None]
    bump = jnp.exp(-(row_gap * row_gap + column_gap * column_gap) / (2.0 * bump_width * bump_width))
    factor_key = jax.random.fold_in(key, 29)
    factor = jax.random.uniform(factor_key, bump.shape, jnp.float32, 0.5, 1.5)
    return (influence_scale * (bump + far_level) * factor).astype(jnp.bfloat16)


def place_ends(drawn, stream_key, smallest, high):
    dims = drawn.shape
    place = [jax.random.randint(jax.random.fold_in(stream_key, axis), (), 0, dims[axis]) for axis in range(len(dims))]
    drawn = drawn.at[tuple(place)].set(smallest)
    longest = dims.index(max(dims))
    place[longest] = (place[longest] + 1) % dims[longest]
    return drawn.at[tuple(place)].set(high)


def block_levels(rng, extent, cuts, least, top_value):
    level, own = 1.0, jax.random.fold_in(rng, 6)
    for axis_at, parts in cuts:
        draws = jnp.exp(jax.random.uniform(jax.random.fold_in(own, axis_at), (parts,), jnp.float32, least / len(cuts), top_value / len(cuts)))
        level = level * jnp.repeat(draws, extent[axis_at] // parts).reshape([-1 if axis == axis_at else 1 for axis in range(len(extent))])
    return level


def setup_inputs(seed: int = 0) -> dict:
    keys = jax.random.split(jax.random.key(seed), 8)
    screens = draw_screens(jax.random.fold_in(keys[7], 71), 0)
    ray_shift = draw_ray_shift(jax.random.fold_in(keys[7], 71), 0)
    ray_weight = jnp.clip(0.5 * jax.random.uniform(keys[2], (DIRS, LAYERS, 4), jnp.float32) ** block_levels(keys[2], (DIRS, LAYERS, 4), ((0, 4),), -0.2, 0.2), 0.0, 0.5)
    influence_index = draw_influence_index(jax.random.fold_in(keys[7], 71), 0)
    influence = draw_influence(jax.random.fold_in(keys[7], 71), 0)
    pupil_mask = place_ends((jax.random.randint(keys[5], (PUPIL, COLS), 0, 5) < 4).astype(jnp.int32), jax.random.fold_in(keys[5], 1), 0, 1)
    petal = place_ends(jax.random.randint(keys[6], (AROWS, ACOLS), 0, 7), jax.random.fold_in(keys[6], 1), 0, 6).astype(jnp.int32)
    return {"screens": screens, "ray_shift": ray_shift, "ray_weight": ray_weight, "influence_index": influence_index, "influence": influence, "pupil_mask": pupil_mask, "petal": petal}


ridge_weight = 1.0
piston_weight = 0.002
highest = lax.Precision.HIGHEST


def trace_one(screens, shifts, layer_gains):
    summed = jnp.zeros((PUPIL, COLS), jnp.float32)
    for layer_index in range(LAYERS):
        shifted = screens[layer_index].astype(jnp.float32)
        shifted = jnp.roll(shifted, -shifts[layer_index, 0], axis=0)
        shifted = jnp.roll(shifted, -shifts[layer_index, 1], axis=1)
        beside = jnp.roll(shifted, -1, axis=1)
        lower_row = jnp.roll(shifted, -1, axis=0)
        corner = jnp.roll(beside, -1, axis=0)
        gains = layer_gains[layer_index]
        summed = summed + (gains[0] * shifted + gains[1] * beside + gains[2] * lower_row + gains[3] * corner)
    return summed


def footprint(influence_index):
    tile_count = COLS_DEV // 128
    band_start = (jnp.arange(PUPIL, dtype=jnp.int32) // ROWS_DEV) * AR_DEV
    block_start = (jnp.arange(COLS // 128, dtype=jnp.int32) // tile_count) * AC_DEV
    grid_row = band_start[:, None, None] + influence_index // (AC_DEV + 2)
    grid_column = block_start[None, :, None] + influence_index % (AC_DEV + 2)
    return grid_row, grid_column


def surface(commands, values, grid_row, grid_column):
    padded = jnp.pad(commands, 1)
    picked = padded[grid_row, grid_column]
    tile_sums = jnp.einsum("rckp,rck->rcp", values, picked, precision=highest)
    return tile_sums.reshape(PUPIL, COLS)


def transpose_map(field, values, grid_row, grid_column):
    tile_field = field.reshape(PUPIL, COLS // 128, 128)
    tile_terms = jnp.einsum("rckp,rcp->rck", values, tile_field, precision=highest)
    padded = jnp.zeros((AROWS + 2, ACOLS + 2), jnp.float32).at[grid_row, grid_column].add(tile_terms)
    return padded[1:-1, 1:-1]


def reference(screens, ray_shift, ray_weight, influence_index, influence, pupil_mask, petal):
    def accumulate(carried, member):
        return carried + trace_one(screens, member[0], member[1]), None

    summed, _ = lax.scan(accumulate, jnp.zeros((PUPIL, COLS), jnp.float32), (ray_shift, ray_weight))
    mean_phase = summed / DIRS
    values = influence.astype(jnp.float32)
    grid_row, grid_column = footprint(influence_index)
    weights = pupil_mask.astype(jnp.float32)
    active = (petal < 6).astype(jnp.float32)
    petals = (petal[:, :, None] == jnp.arange(6, dtype=jnp.int32)[None, None, :]).astype(jnp.float32)

    def operator(vector):
        local_part = active * transpose_map(weights * surface(vector, values, grid_row, grid_column), values, grid_row, grid_column) + ridge_weight * vector
        petal_totals = jnp.einsum("ijp,ij->p", petals, vector, precision=highest)
        return local_part + piston_weight * jnp.einsum("ijp,p->ij", petals, petal_totals, precision=highest)

    rhs = active * transpose_map(weights * mean_phase, values, grid_row, grid_column)
    commands = jnp.zeros_like(rhs)
    residual = rhs
    direction = rhs
    norm_now = jnp.sum(residual * residual)
    for step_index in range(ITERS):
        applied = operator(direction)
        step_size = norm_now / jnp.sum(direction * applied)
        commands = commands + step_size * direction
        residual = residual - step_size * applied
        norm_next = jnp.sum(residual * residual)
        direction = residual + (norm_next / norm_now) * direction
        norm_now = norm_next
    fitted = surface(commands, values, grid_row, grid_column)

    def correct(member):
        return (trace_one(screens, member[0], member[1]) - fitted).astype(jnp.bfloat16)

    corrected = lax.map(correct, (ray_shift, ray_weight))
    return commands, corrected
```

```python
import jax
import jax.numpy as jnp
from jax import lax
from jax.sharding import PartitionSpec as P

SPAN = 2
AR_DEV = 3
AC_DEV = 12
ITERS = 3


ridge_weight = 1.0
piston_weight = 0.002
highest = lax.Precision.HIGHEST


def passed_along(array, axis, by):
    size = lax.axis_size(axis)
    return lax.ppermute(array, axis, [(i, (i + by) % size) for i in range(size)])


def band_stack_whole(piece):
    bands = []
    for offset in range(SPAN, -SPAN - 1, -1):
        if offset == 0:
            bands.append(piece)
        else:
            bands.append(passed_along(piece, "tile", offset))
    return jnp.concatenate(bands, axis=1)


def trace_rows(padded_rim, shifts, layer_gains, rim_depth, band_rows):
    summed = jnp.zeros((band_rows, padded_rim.shape[2]), jnp.float32)
    for layer_index in range(padded_rim.shape[0]):
        window = lax.dynamic_slice_in_dim(
            padded_rim[layer_index], rim_depth + shifts[layer_index, 0], band_rows + 1, 0
        ).astype(jnp.float32)
        window = jnp.roll(window, -shifts[layer_index, 1], axis=1)
        beside = jnp.roll(window, -1, axis=1)
        gains = layer_gains[layer_index]
        summed = summed + (
            gains[0] * window[:-1]
            + gains[1] * beside[:-1]
            + gains[2] * window[1:]
            + gains[3] * beside[1:]
        )
    return summed


def windows(array, axis, count, stride, width):
    parts = [
        lax.slice_in_dim(array, offset, offset + stride * (count - 1) + 1, stride=stride, axis=axis)
        for offset in range(width)
    ]
    return jnp.stack(parts, axis=axis + 1)


def on_device(screens, ray_shift, ray_weight, influence_index, influence, pupil_mask, petal):
    band_rows = screens.shape[1]
    rim_depth = SPAN * band_rows
    padded_rim = band_stack_whole(screens)
    phases = [
        trace_rows(padded_rim, ray_shift[member], ray_weight[member], rim_depth, band_rows)
        for member in range(ray_shift.shape[0])
    ]
    tile_count = lax.axis_size("tile")
    dir_count = lax.axis_size("dir")
    direction_count = ray_shift.shape[0] * dir_count
    summed = phases[0]
    for member in range(1, len(phases)):
        summed = summed + phases[member]
    mean_phase = (
        lax.psum_scatter(
            summed.astype(jnp.bfloat16), "dir", scatter_dimension=1, tiled=True
        ).astype(jnp.float32)
        / direction_count
    )
    tiles_here = influence.shape[1]
    near_count = influence.shape[2]
    block_rows, block_columns = petal.shape
    ext_rows, ext_columns = block_rows + 2, block_columns + 2
    extent = ext_rows * ext_columns
    values = influence.astype(jnp.float32)
    onehot = (influence_index[..., None] == jnp.arange(extent, dtype=jnp.int32)).astype(
        jnp.float32
    )
    weights = pupil_mask.astype(jnp.float32).reshape(band_rows, tiles_here, 128)

    masked = (influence * weights[:, :, None, :].astype(jnp.bfloat16))
    gram = jnp.einsum(
        "rckp,rcjp->rckj", masked, influence, preferred_element_type=jnp.float32
    )
    placed = jnp.einsum("rckj,rcjb->rckb", gram, onehot, precision=highest)
    block_matrix = jnp.einsum("rcka,rckb->ab", onehot, placed, precision=highest)

    field = (weights * mean_phase.reshape(band_rows, tiles_here, 128))
    tile_terms = jnp.einsum("rckp,rcp->rck", values, field, precision=highest)
    block_rhs = jnp.einsum("rck,rcka->a", tile_terms, onehot, precision=highest)

    payload = jnp.concatenate(
        [block_matrix.reshape(-1), block_rhs, petal.reshape(-1).astype(jnp.float32)]
    )
    gathered = lax.all_gather(payload, ("tile", "dir"), tiled=False)
    block_count = tile_count * dir_count
    matrices = gathered[:, : extent * extent].reshape(block_count, extent, extent)
    rhs_blocks = gathered[:, extent * extent : extent * extent + extent]
    petal_blocks = gathered[:, extent * extent + extent :].reshape(
        tile_count, dir_count, block_rows, block_columns
    )
    grid_rows, grid_columns = tile_count * block_rows, dir_count * block_columns
    petal_grid = petal_blocks.transpose(0, 2, 1, 3).reshape(grid_rows, grid_columns)
    active = (petal_grid < 6).astype(jnp.float32)
    petals = (petal_grid[:, :, None] == jnp.arange(6, dtype=jnp.float32)).astype(jnp.float32)

    def gather_blocks(padded):
        rows = windows(padded, 0, tile_count, block_rows, ext_rows)
        both = windows(rows, 2, dir_count, block_columns, ext_columns)
        return both.transpose(0, 2, 1, 3).reshape(block_count, extent)

    padded_shape = jax.ShapeDtypeStruct((grid_rows + 2, grid_columns + 2), jnp.float32)
    scatter_blocks = jax.linear_transpose(gather_blocks, padded_shape)

    def spread_blocks(blocks):
        (padded,) = scatter_blocks(blocks)
        return padded[1:-1, 1:-1]

    def operator(vector):
        picked = gather_blocks(jnp.pad(vector, 1))
        terms = jnp.einsum("bij,bj->bi", matrices, picked, precision=highest)
        local_part = active * spread_blocks(terms) + ridge_weight * vector
        petal_totals = jnp.einsum("ijp,ij->p", petals, vector, precision=highest)
        return local_part + piston_weight * jnp.einsum(
            "ijp,p->ij", petals, petal_totals, precision=highest
        )

    rhs = active * spread_blocks(rhs_blocks)
    commands = jnp.zeros_like(rhs)
    residual = rhs
    direction = rhs
    norm_now = jnp.sum(residual * residual)
    for step_index in range(ITERS):
        applied = operator(direction)
        step_size = norm_now / jnp.sum(direction * applied)
        commands = commands + step_size * direction
        residual = residual - step_size * applied
        norm_next = jnp.sum(residual * residual)
        direction = residual + (norm_next / norm_now) * direction
        norm_now = norm_next

    row_at = lax.axis_index("tile") * block_rows
    column_at = lax.axis_index("dir") * block_columns
    own = lax.dynamic_slice(commands, (row_at, column_at), (block_rows, block_columns))
    extended = lax.dynamic_slice(
        jnp.pad(commands, 1), (row_at, column_at), (ext_rows, ext_columns)
    )
    picked = jnp.einsum("rcka,a->rck", onehot, extended.reshape(-1), precision=highest)
    fitted = jnp.einsum("rckp,rck->rcp", values, picked, precision=highest).reshape(
        band_rows, tiles_here * 128
    )
    whole_band = lax.all_gather(fitted.astype(jnp.bfloat16), "dir", axis=1, tiled=True).astype(
        fitted.dtype
    )
    corrected = jnp.stack([(phase_rows - whole_band).astype(jnp.bfloat16) for phase_rows in phases])
    return (own, corrected)


def solution(mesh):
    in_specs = (
        P(None, "tile", None),
        P("dir", None, None),
        P("dir", None, None),
        P("tile", "dir", None),
        P("tile", "dir", None, None),
        P("tile", "dir"),
        P("tile", "dir"),
    )
    out_specs = (P("tile", "dir"), P("dir", "tile", None))
    return jax.shard_map(
        on_device, mesh=mesh, in_specs=in_specs, out_specs=out_specs, check_vma=False
    )
```

```python
import jax
import numpy as np
import jax.numpy as jnp
from jax import lax
from jax.sharding import PartitionSpec as P

SPAN = 2
AR_DEV = 3
AC_DEV = 12
ITERS = 3


ridge_weight = 1.0
piston_weight = 0.002
highest = lax.Precision.HIGHEST


def passed_along(array, axis, by):
    size = lax.axis_size(axis)
    return lax.ppermute(array, axis, [(i, (i + by) % size) for i in range(size)])


def band_stack_whole(piece):
    bands = []
    for offset in range(SPAN, -SPAN - 1, -1):
        if offset == 0:
            bands.append(piece)
        else:
            bands.append(passed_along(piece, "tile", offset))
    return jnp.concatenate(bands, axis=1)


def trace_rows(padded_rim, shifts, layer_gains, rim_depth, band_rows):
    summed = jnp.zeros((band_rows, padded_rim.shape[2]), jnp.float32)
    for layer_index in range(padded_rim.shape[0]):
        window = lax.dynamic_slice_in_dim(
            padded_rim[layer_index], rim_depth + shifts[layer_index, 0], band_rows + 1, 0
        ).astype(jnp.float32)
        window = jnp.roll(window, -shifts[layer_index, 1], axis=1)
        beside = jnp.roll(window, -1, axis=1)
        gains = layer_gains[layer_index]
        summed = summed + (
            gains[0] * window[:-1]
            + gains[1] * beside[:-1]
            + gains[2] * window[1:]
            + gains[3] * beside[1:]
        )
    return summed


def windows(array, axis, count, stride, width):
    parts = [
        lax.slice_in_dim(array, offset, offset + stride * (count - 1) + 1, stride=stride, axis=axis)
        for offset in range(width)
    ]
    return jnp.stack(parts, axis=axis + 1)


def on_device(screens, ray_shift, ray_weight, influence_index, influence, pupil_mask, petal):
    band_rows = screens.shape[1]
    rim_depth = SPAN * band_rows
    padded_rim = band_stack_whole(screens)
    phases = [
        trace_rows(padded_rim, ray_shift[member], ray_weight[member], rim_depth, band_rows)
        for member in range(ray_shift.shape[0])
    ]
    tile_count = lax.axis_size("tile")
    dir_count = lax.axis_size("dir")
    direction_count = ray_shift.shape[0] * dir_count
    summed = phases[0]
    for member in range(1, len(phases)):
        summed = summed + phases[member]
    mean_phase = (
        lax.psum_scatter(
            summed.astype(jnp.bfloat16), "dir", scatter_dimension=1, tiled=True
        ).astype(jnp.float32)
        / direction_count
    )
    tiles_here = influence.shape[1]
    near_count = influence.shape[2]
    block_rows, block_columns = petal.shape
    ext_rows, ext_columns = block_rows + 2, block_columns + 2
    extent = ext_rows * ext_columns
    values = influence.astype(jnp.float32)
    onehot = (influence_index[..., None] == jnp.arange(extent, dtype=jnp.int32)).astype(
        jnp.float32
    )
    weights = pupil_mask.astype(jnp.float32).reshape(band_rows, tiles_here, 128)

    masked = (influence * weights[:, :, None, :].astype(jnp.bfloat16))
    gram = jnp.einsum(
        "rckp,rcjp->rckj", masked, influence, preferred_element_type=jnp.float32
    )
    placed = jnp.einsum("rckj,rcjb->rckb", gram, onehot, precision=highest)
    block_matrix = jnp.einsum("rcka,rckb->ab", onehot, placed, precision=highest)

    field = (weights * mean_phase.reshape(band_rows, tiles_here, 128))
    tile_terms = jnp.einsum("rckp,rcp->rck", values, field, precision=highest)
    block_rhs = jnp.einsum("rck,rcka->a", tile_terms, onehot, precision=highest)

    upper_rows, upper_columns = np.triu_indices(extent)
    early = jnp.concatenate(
        [block_matrix[upper_rows, upper_columns], petal.reshape(-1).astype(jnp.float32)]
    )
    block_count = tile_count * dir_count
    slot = lax.axis_index("tile") * dir_count + lax.axis_index("dir")
    early = lax.psum(
        lax.dynamic_update_slice(
            jnp.zeros((block_count, early.shape[0]), jnp.float32), early[None], (slot, 0)
        ),
        ("tile", "dir"),
    )
    upper_count = upper_rows.shape[0]
    halves = jnp.zeros((block_count, extent, extent), jnp.float32).at[
        :, upper_rows, upper_columns
    ].set(early[:, :upper_count])
    diagonal = jnp.eye(extent, dtype=jnp.float32)
    matrices = halves + jnp.swapaxes(halves, 1, 2) * (1.0 - diagonal)
    petal_blocks = early[:, upper_count:].reshape(
        tile_count, dir_count, block_rows, block_columns
    )
    late = lax.dynamic_update_slice(
        jnp.zeros((block_count, extent), jnp.float32), block_rhs[None], (slot, 0)
    )
    rhs_blocks = lax.psum(late + 0.0 * early[0, 0], ("tile", "dir"))
    grid_rows, grid_columns = tile_count * block_rows, dir_count * block_columns
    petal_grid = petal_blocks.transpose(0, 2, 1, 3).reshape(grid_rows, grid_columns)
    active = (petal_grid < 6).astype(jnp.float32)
    petals = (petal_grid[:, :, None] == jnp.arange(6, dtype=jnp.float32)).astype(jnp.float32)

    def gather_blocks(padded):
        rows = windows(padded, 0, tile_count, block_rows, ext_rows)
        both = windows(rows, 2, dir_count, block_columns, ext_columns)
        return both.transpose(0, 2, 1, 3).reshape(block_count, extent)

    padded_shape = jax.ShapeDtypeStruct((grid_rows + 2, grid_columns + 2), jnp.float32)
    scatter_blocks = jax.linear_transpose(gather_blocks, padded_shape)

    def spread_blocks(blocks):
        (padded,) = scatter_blocks(blocks)
        return padded[1:-1, 1:-1]

    def operator(vector):
        picked = gather_blocks(jnp.pad(vector, 1))
        terms = jnp.einsum("bij,bj->bi", matrices, picked, precision=highest)
        local_part = active * spread_blocks(terms) + ridge_weight * vector
        petal_totals = jnp.einsum("ijp,ij->p", petals, vector, precision=highest)
        return local_part + piston_weight * jnp.einsum(
            "ijp,p->ij", petals, petal_totals, precision=highest
        )

    rhs = active * spread_blocks(rhs_blocks)
    commands = jnp.zeros_like(rhs)
    residual = rhs
    direction = rhs
    norm_now = jnp.sum(residual * residual)
    for step_index in range(ITERS):
        applied = operator(direction)
        step_size = norm_now / jnp.sum(direction * applied)
        commands = commands + step_size * direction
        residual = residual - step_size * applied
        norm_next = jnp.sum(residual * residual)
        direction = residual + (norm_next / norm_now) * direction
        norm_now = norm_next

    row_at = lax.axis_index("tile") * block_rows
    column_at = lax.axis_index("dir") * block_columns
    own = lax.dynamic_slice(commands, (row_at, column_at), (block_rows, block_columns))
    extended = lax.dynamic_slice(
        jnp.pad(commands, 1), (row_at, column_at), (ext_rows, ext_columns)
    )
    picked = jnp.einsum("rcka,a->rck", onehot, extended.reshape(-1), precision=highest)
    fitted = jnp.einsum("rckp,rck->rcp", values, picked, precision=highest).reshape(
        band_rows, tiles_here * 128
    )
    whole_band = lax.all_gather(fitted.astype(jnp.bfloat16), "dir", axis=1, tiled=True).astype(
        fitted.dtype
    )
    corrected = jnp.stack([(phase_rows - whole_band).astype(jnp.bfloat16) for phase_rows in phases])
    return (own, corrected)


def solution(mesh):
    in_specs = (
        P(None, "tile", None),
        P("dir", None, None),
        P("dir", None, None),
        P("tile", "dir", None),
        P("tile", "dir", None, None),
        P("tile", "dir"),
        P("tile", "dir"),
    )
    out_specs = (P("tile", "dir"), P("dir", "tile", None))
    return jax.shard_map(
        on_device, mesh=mesh, in_specs=in_specs, out_specs=out_specs, check_vma=False
    )
```

```python
import jax
import numpy as np
import jax.numpy as jnp
from jax import lax
from jax.experimental import pallas as pl
from jax.experimental.pallas import tpu as pltpu
from jax.sharding import PartitionSpec as P

SPAN = 2
AR_DEV = 3
AC_DEV = 12
ITERS = 3


ridge_weight = 1.0
piston_weight = 0.002
highest = lax.Precision.HIGHEST


def passed_along(array, axis, by):
    size = lax.axis_size(axis)
    return lax.ppermute(array, axis, [(i, (i + by) % size) for i in range(size)])


def band_stack_whole(piece):
    bands = []
    for offset in range(SPAN, -SPAN - 1, -1):
        if offset == 0:
            bands.append(piece)
        else:
            bands.append(passed_along(piece, "tile", offset))
    return jnp.concatenate(bands, axis=1)


def trace_kernel(shift_ref, gain_ref, rim_ref, phase_ref):
    member = pl.program_id(0)
    layers, rim_rows, columns = rim_ref.shape
    band_rows = phase_ref.shape[1]
    rim_depth = (rim_rows - band_rows) // 2
    chunk_rows = band_rows + 16
    total = jnp.zeros((band_rows, columns), jnp.float32)
    row_index = lax.broadcasted_iota(jnp.int32, (band_rows, chunk_rows), 0)
    chunk_index = lax.broadcasted_iota(jnp.int32, (band_rows, chunk_rows), 1)
    for layer_index in range(layers):
        first = rim_depth + shift_ref[member, layer_index, 0]
        start = jnp.clip((first // 16) * 16, 0, rim_rows - chunk_rows)
        start = pl.multiple_of(start, 16)
        lead = first - start
        chunk = rim_ref[layer_index, pl.ds(start, chunk_rows), :].astype(jnp.float32)
        turn = (columns - lax.rem(shift_ref[member, layer_index, 1], columns)) % columns
        window = pltpu.roll(chunk, turn, 1)
        beside = pltpu.roll(window, columns - 1, 1)
        upper = (chunk_index == row_index + lead).astype(jnp.bfloat16)
        lower = (chunk_index == row_index + lead + 1).astype(jnp.bfloat16)
        window = window.astype(jnp.bfloat16)
        beside = beside.astype(jnp.bfloat16)
        top = jnp.dot(upper, window, preferred_element_type=jnp.float32)
        top_beside = jnp.dot(upper, beside, preferred_element_type=jnp.float32)
        bottom = jnp.dot(lower, window, preferred_element_type=jnp.float32)
        bottom_beside = jnp.dot(lower, beside, preferred_element_type=jnp.float32)
        total = total + (
            gain_ref[member, layer_index, 0] * top
            + gain_ref[member, layer_index, 1] * top_beside
            + gain_ref[member, layer_index, 2] * bottom
            + gain_ref[member, layer_index, 3] * bottom_beside
        )
    phase_ref[0] = total


def trace_all(padded_rim, ray_shift, ray_weight, band_rows):
    layers, rim_rows, columns = padded_rim.shape
    members = ray_shift.shape[0]
    return pl.pallas_call(
        trace_kernel,
        out_shape=jax.ShapeDtypeStruct((members, band_rows, columns), jnp.float32),
        grid=(members,),
        in_specs=[
            pl.BlockSpec(memory_space=pltpu.SMEM),
            pl.BlockSpec(memory_space=pltpu.SMEM),
            pl.BlockSpec((layers, rim_rows, columns), lambda m: (0, 0, 0)),
        ],
        out_specs=pl.BlockSpec((1, band_rows, columns), lambda m: (m, 0, 0)),
        compiler_params=pltpu.CompilerParams(vmem_limit_bytes=48 * 1024 * 1024),
    )(ray_shift, ray_weight, padded_rim)


def windows(array, axis, count, stride, width):
    parts = [
        lax.slice_in_dim(array, offset, offset + stride * (count - 1) + 1, stride=stride, axis=axis)
        for offset in range(width)
    ]
    return jnp.stack(parts, axis=axis + 1)


def on_device(screens, ray_shift, ray_weight, influence_index, influence, pupil_mask, petal):
    band_rows = screens.shape[1]
    padded_rim = band_stack_whole(screens)
    phases = trace_all(padded_rim, ray_shift, ray_weight, band_rows)
    tile_count = lax.axis_size("tile")
    dir_count = lax.axis_size("dir")
    direction_count = ray_shift.shape[0] * dir_count
    summed = jnp.sum(phases, axis=0)
    mean_phase = (
        lax.psum_scatter(
            summed.astype(jnp.bfloat16), "dir", scatter_dimension=1, tiled=True
        ).astype(jnp.float32)
        / direction_count
    )
    tiles_here = influence.shape[1]
    near_count = influence.shape[2]
    block_rows, block_columns = petal.shape
    ext_rows, ext_columns = block_rows + 2, block_columns + 2
    extent = ext_rows * ext_columns
    values = influence.astype(jnp.float32)
    onehot = (influence_index[..., None] == jnp.arange(extent, dtype=jnp.int32)).astype(
        jnp.float32
    )
    weights = pupil_mask.astype(jnp.float32).reshape(band_rows, tiles_here, 128)

    masked = (influence * weights[:, :, None, :].astype(jnp.bfloat16))
    gram = jnp.einsum(
        "rckp,rcjp->rckj", masked, influence, preferred_element_type=jnp.float32
    )
    placed = jnp.einsum("rckj,rcjb->rckb", gram, onehot, precision=highest)
    block_matrix = jnp.einsum("rcka,rckb->ab", onehot, placed, precision=highest)

    field = (weights * mean_phase.reshape(band_rows, tiles_here, 128))
    tile_terms = jnp.einsum("rckp,rcp->rck", values, field, precision=highest)
    block_rhs = jnp.einsum("rck,rcka->a", tile_terms, onehot, precision=highest)

    early = jnp.concatenate([block_matrix.reshape(-1), petal.reshape(-1).astype(jnp.float32)])
    block_count = tile_count * dir_count
    slot = lax.axis_index("tile") * dir_count + lax.axis_index("dir")
    early = lax.psum(
        lax.dynamic_update_slice(
            jnp.zeros((block_count, early.shape[0]), jnp.float32), early[None], (slot, 0)
        ),
        ("tile", "dir"),
    )
    matrices = early[:, : extent * extent].reshape(block_count, extent, extent)
    petal_blocks = early[:, extent * extent :].reshape(
        tile_count, dir_count, block_rows, block_columns
    )
    late = lax.dynamic_update_slice(
        jnp.zeros((block_count, extent), jnp.float32), block_rhs[None], (slot, 0)
    )
    rhs_blocks = lax.psum(late + 0.0 * early[0, 0], ("tile", "dir"))
    grid_rows, grid_columns = tile_count * block_rows, dir_count * block_columns
    petal_grid = petal_blocks.transpose(0, 2, 1, 3).reshape(grid_rows, grid_columns)
    active = (petal_grid < 6).astype(jnp.float32)
    petals = (petal_grid[:, :, None] == jnp.arange(6, dtype=jnp.float32)).astype(jnp.float32)

    def gather_blocks(padded):
        rows = windows(padded, 0, tile_count, block_rows, ext_rows)
        both = windows(rows, 2, dir_count, block_columns, ext_columns)
        return both.transpose(0, 2, 1, 3).reshape(block_count, extent)

    padded_shape = jax.ShapeDtypeStruct((grid_rows + 2, grid_columns + 2), jnp.float32)
    scatter_blocks = jax.linear_transpose(gather_blocks, padded_shape)

    def spread_blocks(blocks):
        (padded,) = scatter_blocks(blocks)
        return padded[1:-1, 1:-1]

    def operator(vector):
        picked = gather_blocks(jnp.pad(vector, 1))
        terms = jnp.einsum("bij,bj->bi", matrices, picked, precision=highest)
        local_part = active * spread_blocks(terms) + ridge_weight * vector
        petal_totals = jnp.einsum("ijp,ij->p", petals, vector, precision=highest)
        return local_part + piston_weight * jnp.einsum(
            "ijp,p->ij", petals, petal_totals, precision=highest
        )

    rhs = active * spread_blocks(rhs_blocks)
    commands = jnp.zeros_like(rhs)
    residual = rhs
    direction = rhs
    norm_now = jnp.sum(residual * residual)
    for step_index in range(ITERS):
        applied = operator(direction)
        step_size = norm_now / jnp.sum(direction * applied)
        commands = commands + step_size * direction
        residual = residual - step_size * applied
        norm_next = jnp.sum(residual * residual)
        direction = residual + (norm_next / norm_now) * direction
        norm_now = norm_next

    row_at = lax.axis_index("tile") * block_rows
    column_at = lax.axis_index("dir") * block_columns
    own = lax.dynamic_slice(commands, (row_at, column_at), (block_rows, block_columns))
    extended = lax.dynamic_slice(
        jnp.pad(commands, 1), (row_at, column_at), (ext_rows, ext_columns)
    )
    picked = jnp.einsum("rcka,a->rck", onehot, extended.reshape(-1), precision=highest)
    fitted = jnp.einsum("rckp,rck->rcp", values, picked, precision=highest).reshape(
        band_rows, tiles_here * 128
    )
    whole_band = lax.all_gather(fitted.astype(jnp.bfloat16), "dir", axis=1, tiled=True).astype(
        fitted.dtype
    )
    corrected = (phases - whole_band[None]).astype(jnp.bfloat16)
    return (own, corrected)


def solution(mesh):
    in_specs = (
        P(None, "tile", None),
        P("dir", None, None),
        P("dir", None, None),
        P("tile", "dir", None),
        P("tile", "dir", None, None),
        P("tile", "dir"),
        P("tile", "dir"),
    )
    out_specs = (P("tile", "dir"), P("dir", "tile", None))
    return jax.shard_map(
        on_device, mesh=mesh, in_specs=in_specs, out_specs=out_specs, check_vma=False
    )
```

```python
import jax
import numpy as np
import jax.numpy as jnp
from jax import lax
from jax.experimental import pallas as pl
from jax.experimental.pallas import tpu as pltpu
from jax.sharding import PartitionSpec as P

SPAN = 2
AR_DEV = 3
AC_DEV = 12
ITERS = 3


ridge_weight = 1.0
piston_weight = 0.002
highest = lax.Precision.HIGHEST


def passed_along(array, axis, by):
    size = lax.axis_size(axis)
    return lax.ppermute(array, axis, [(i, (i + by) % size) for i in range(size)])


def band_stack_whole(piece):
    bands = []
    for offset in range(SPAN, -SPAN - 1, -1):
        if offset == 0:
            bands.append(piece)
        else:
            bands.append(passed_along(piece, "tile", offset))
    return jnp.concatenate(bands, axis=1)


def trace_kernel(shift_ref, gain_ref, rim_ref, phase_ref):
    member = pl.program_id(0)
    layers, rim_rows, columns = rim_ref.shape
    band_rows = phase_ref.shape[1]
    rim_depth = (rim_rows - band_rows) // 2
    chunk_rows = band_rows + 16
    total = jnp.zeros((band_rows, columns), jnp.float32)
    row_index = lax.broadcasted_iota(jnp.int32, (band_rows, chunk_rows), 0)
    chunk_index = lax.broadcasted_iota(jnp.int32, (band_rows, chunk_rows), 1)
    for layer_index in range(layers):
        first = rim_depth + shift_ref[member, layer_index, 0]
        start = jnp.clip((first // 16) * 16, 0, rim_rows - chunk_rows)
        start = pl.multiple_of(start, 16)
        lead = first - start
        chunk = rim_ref[layer_index, pl.ds(start, chunk_rows), :].astype(jnp.float32)
        turn = (columns - lax.rem(shift_ref[member, layer_index, 1], columns)) % columns
        window = pltpu.roll(chunk, turn, 1)
        beside = pltpu.roll(window, columns - 1, 1)
        upper = (chunk_index == row_index + lead).astype(jnp.bfloat16)
        lower = (chunk_index == row_index + lead + 1).astype(jnp.bfloat16)
        window = window.astype(jnp.bfloat16)
        beside = beside.astype(jnp.bfloat16)
        top = jnp.dot(upper, window, preferred_element_type=jnp.float32)
        top_beside = jnp.dot(upper, beside, preferred_element_type=jnp.float32)
        bottom = jnp.dot(lower, window, preferred_element_type=jnp.float32)
        bottom_beside = jnp.dot(lower, beside, preferred_element_type=jnp.float32)
        total = total + (
            gain_ref[member, layer_index, 0] * top
            + gain_ref[member, layer_index, 1] * top_beside
            + gain_ref[member, layer_index, 2] * bottom
            + gain_ref[member, layer_index, 3] * bottom_beside
        )
    phase_ref[0] = total


def trace_all(padded_rim, ray_shift, ray_weight, band_rows):
    layers, rim_rows, columns = padded_rim.shape
    members = ray_shift.shape[0]
    return pl.pallas_call(
        trace_kernel,
        out_shape=jax.ShapeDtypeStruct((members, band_rows, columns), jnp.float32),
        grid=(members,),
        in_specs=[
            pl.BlockSpec(memory_space=pltpu.SMEM),
            pl.BlockSpec(memory_space=pltpu.SMEM),
            pl.BlockSpec((layers, rim_rows, columns), lambda m: (0, 0, 0)),
        ],
        out_specs=pl.BlockSpec((1, band_rows, columns), lambda m: (m, 0, 0)),
        compiler_params=pltpu.CompilerParams(vmem_limit_bytes=48 * 1024 * 1024),
    )(ray_shift, ray_weight, padded_rim)


def windows(array, axis, count, stride, width):
    parts = [
        lax.slice_in_dim(array, offset, offset + stride * (count - 1) + 1, stride=stride, axis=axis)
        for offset in range(width)
    ]
    return jnp.stack(parts, axis=axis + 1)


def pack_symmetric(matrix):
    half = matrix.shape[0] // 2
    first, across, last = matrix[:half, :half], matrix[:half, half:], matrix[half:, half:]
    row = lax.broadcasted_iota(jnp.int32, (half, half + 1), 0)
    column = lax.broadcasted_iota(jnp.int32, (half, half + 1), 1)
    folded = jnp.where(
        column <= row, jnp.pad(last, ((0, 0), (0, 1))), jnp.pad(first, ((0, 0), (1, 0)))
    )
    return jnp.concatenate([folded.reshape(-1), across.reshape(-1)])


def unpack_symmetric(packed, extent):
    half = extent // 2
    folded = packed[: half * (half + 1)].reshape(half, half + 1)
    across = packed[half * (half + 1) :].reshape(half, half)
    row = lax.broadcasted_iota(jnp.int32, (half, half), 0)
    column = lax.broadcasted_iota(jnp.int32, (half, half), 1)
    last = jnp.where(column <= row, folded[:, :half], 0.0)
    first = jnp.where(column >= row, folded[:, 1:], 0.0)
    diagonal = (row == column).astype(jnp.float32)
    first = first + first.T * (1.0 - diagonal)
    last = last + last.T * (1.0 - diagonal)
    return jnp.concatenate(
        [jnp.concatenate([first, across], axis=1), jnp.concatenate([across.T, last], axis=1)],
        axis=0,
    )


def doubling_sum(value, axes):
    for axis, size in axes:
        step = 1
        while step < size:
            pairs = [(i, i ^ step) for i in range(size)]
            value = value + lax.ppermute(value, axis, pairs)
            step *= 2
    return value


def on_device(screens, ray_shift, ray_weight, influence_index, influence, pupil_mask, petal):
    band_rows = screens.shape[1]
    padded_rim = band_stack_whole(screens)
    phases = trace_all(padded_rim, ray_shift, ray_weight, band_rows)
    tile_count = lax.axis_size("tile")
    dir_count = lax.axis_size("dir")
    direction_count = ray_shift.shape[0] * dir_count
    summed = jnp.sum(phases, axis=0)
    mean_phase = (
        lax.psum_scatter(
            summed.astype(jnp.bfloat16), "dir", scatter_dimension=1, tiled=True
        ).astype(jnp.float32)
        / direction_count
    )
    tiles_here = influence.shape[1]
    near_count = influence.shape[2]
    block_rows, block_columns = petal.shape
    ext_rows, ext_columns = block_rows + 2, block_columns + 2
    extent = ext_rows * ext_columns
    values = influence.astype(jnp.float32)
    onehot = (influence_index[..., None] == jnp.arange(extent, dtype=jnp.int32)).astype(
        jnp.float32
    )
    weights = pupil_mask.astype(jnp.float32).reshape(band_rows, tiles_here, 128)

    masked = (influence * weights[:, :, None, :].astype(jnp.bfloat16))
    gram = jnp.einsum(
        "rckp,rcjp->rckj", masked, influence, preferred_element_type=jnp.float32
    )
    placed = jnp.einsum("rckj,rcjb->rckb", gram, onehot, precision=highest)
    block_matrix = jnp.einsum("rcka,rckb->ab", onehot, placed, precision=highest)

    field = (weights * mean_phase.reshape(band_rows, tiles_here, 128))
    tile_terms = jnp.einsum("rckp,rcp->rck", values, field, precision=highest)
    block_rhs = jnp.einsum("rck,rcka->a", tile_terms, onehot, precision=highest)

    early = jnp.concatenate([pack_symmetric(block_matrix), petal.reshape(-1).astype(jnp.float32)])
    block_count = tile_count * dir_count
    slot = lax.axis_index("tile") * dir_count + lax.axis_index("dir")
    early = lax.psum(
        lax.dynamic_update_slice(
            jnp.zeros((block_count, early.shape[0]), jnp.float32), early[None], (slot, 0)
        ),
        ("tile", "dir"),
    )
    packed_count = extent * extent // 2 + extent // 2
    matrices = jax.vmap(lambda packed: unpack_symmetric(packed, extent))(early[:, :packed_count])
    petal_blocks = early[:, packed_count:].reshape(
        tile_count, dir_count, block_rows, block_columns
    )
    late = lax.dynamic_update_slice(
        jnp.zeros((block_count, extent), jnp.float32), block_rhs[None], (slot, 0)
    )
    rhs_blocks = doubling_sum(late + 0.0 * early[0, 0], (("dir", dir_count), ("tile", tile_count)))
    grid_rows, grid_columns = tile_count * block_rows, dir_count * block_columns
    petal_grid = petal_blocks.transpose(0, 2, 1, 3).reshape(grid_rows, grid_columns)
    active = (petal_grid < 6).astype(jnp.float32)
    petals = (petal_grid[:, :, None] == jnp.arange(6, dtype=jnp.float32)).astype(jnp.float32)

    padded_rows, padded_columns = grid_rows + 2, grid_columns + 2
    row_pick = (
        lax.broadcasted_iota(jnp.int32, (tile_count, ext_rows, padded_rows), 2)
        == block_rows * lax.broadcasted_iota(jnp.int32, (tile_count, ext_rows, padded_rows), 0)
        + lax.broadcasted_iota(jnp.int32, (tile_count, ext_rows, padded_rows), 1)
    ).astype(jnp.float32).reshape(tile_count * ext_rows, padded_rows)
    column_pick = (
        lax.broadcasted_iota(jnp.int32, (padded_columns, dir_count, ext_columns), 0)
        == block_columns
        * lax.broadcasted_iota(jnp.int32, (padded_columns, dir_count, ext_columns), 1)
        + lax.broadcasted_iota(jnp.int32, (padded_columns, dir_count, ext_columns), 2)
    ).astype(jnp.float32).reshape(padded_columns, dir_count * ext_columns)
    block_matrices = matrices.reshape(
        tile_count, dir_count, ext_rows, ext_columns, ext_rows, ext_columns
    )

    def gather_blocks(padded):
        rows = jnp.dot(row_pick, padded, precision=highest)
        return jnp.dot(rows, column_pick, precision=highest).reshape(
            tile_count, ext_rows, dir_count, ext_columns
        )

    def spread_blocks(blocks):
        flat = blocks.reshape(tile_count * ext_rows, dir_count * ext_columns)
        rows = jnp.dot(row_pick.T, flat, precision=highest)
        padded = jnp.dot(rows, column_pick.T, precision=highest)
        return padded[1:-1, 1:-1]

    def operator(vector):
        picked = gather_blocks(jnp.pad(vector, 1))
        terms = jnp.einsum("tdklij,tidj->tkdl", block_matrices, picked, precision=highest)
        local_part = active * spread_blocks(terms) + ridge_weight * vector
        petal_totals = jnp.einsum("ijp,ij->p", petals, vector, precision=highest)
        return local_part + piston_weight * jnp.einsum(
            "ijp,p->ij", petals, petal_totals, precision=highest
        )

    rhs = active * spread_blocks(
        rhs_blocks.reshape(tile_count, dir_count, ext_rows, ext_columns).transpose(0, 2, 1, 3)
    )
    commands = jnp.zeros_like(rhs)
    residual = rhs
    direction = rhs
    norm_now = jnp.sum(residual * residual)
    for step_index in range(ITERS):
        applied = operator(direction)
        step_size = norm_now / jnp.sum(direction * applied)
        commands = commands + step_size * direction
        residual = residual - step_size * applied
        norm_next = jnp.sum(residual * residual)
        direction = residual + (norm_next / norm_now) * direction
        norm_now = norm_next

    row_at = lax.axis_index("tile") * block_rows
    column_at = lax.axis_index("dir") * block_columns
    own = lax.dynamic_slice(commands, (row_at, column_at), (block_rows, block_columns))
    extended = lax.dynamic_slice(
        jnp.pad(commands, 1), (row_at, column_at), (ext_rows, ext_columns)
    )
    picked = jnp.einsum("rcka,a->rck", onehot, extended.reshape(-1), precision=highest)
    fitted = jnp.einsum("rckp,rck->rcp", values, picked, precision=highest).reshape(
        band_rows, tiles_here * 128
    )
    whole_band = lax.all_gather(fitted.astype(jnp.bfloat16), "dir", axis=1, tiled=True).astype(
        fitted.dtype
    )
    corrected = (phases - whole_band[None]).astype(jnp.bfloat16)
    return (own, corrected)


def solution(mesh):
    in_specs = (
        P(None, "tile", None),
        P("dir", None, None),
        P("dir", None, None),
        P("tile", "dir", None),
        P("tile", "dir", None, None),
        P("tile", "dir"),
        P("tile", "dir"),
    )
    out_specs = (P("tile", "dir"), P("dir", "tile", None))
    return jax.shard_map(
        on_device, mesh=mesh, in_specs=in_specs, out_specs=out_specs, check_vma=False
    )
```

```python
import jax
import numpy as np
import jax.numpy as jnp
from jax import lax
from jax.experimental import pallas as pl
from jax.experimental.pallas import tpu as pltpu
from jax.sharding import PartitionSpec as P

SPAN = 2
AR_DEV = 3
AC_DEV = 12
ITERS = 3


ridge_weight = 1.0
piston_weight = 0.002
highest = lax.Precision.HIGHEST


def passed_along(array, axis, by):
    size = lax.axis_size(axis)
    return lax.ppermute(array, axis, [(i, (i + by) % size) for i in range(size)])


def band_stack_whole(piece):
    bands = []
    for offset in range(SPAN, -SPAN - 1, -1):
        if offset == 0:
            bands.append(piece)
        else:
            bands.append(passed_along(piece, "tile", offset))
    return jnp.concatenate(bands, axis=1)


def trace_kernel(shift_ref, gain_ref, rim_ref, phase_ref):
    member = pl.program_id(0)
    layers, rim_rows, columns = rim_ref.shape
    band_rows = phase_ref.shape[1]
    rim_depth = (rim_rows - band_rows) // 2
    chunk_rows = band_rows + 16
    total = jnp.zeros((band_rows, columns), jnp.float32)
    row_index = lax.broadcasted_iota(jnp.int32, (band_rows, chunk_rows), 0)
    chunk_index = lax.broadcasted_iota(jnp.int32, (band_rows, chunk_rows), 1)
    for layer_index in range(layers):
        first = rim_depth + shift_ref[member, layer_index, 0]
        start = jnp.clip((first // 16) * 16, 0, rim_rows - chunk_rows)
        start = pl.multiple_of(start, 16)
        lead = first - start
        chunk = rim_ref[layer_index, pl.ds(start, chunk_rows), :].astype(jnp.float32)
        turn = (columns - lax.rem(shift_ref[member, layer_index, 1], columns)) % columns
        window = pltpu.roll(chunk, turn, 1)
        beside = pltpu.roll(window, columns - 1, 1)
        upper = (chunk_index == row_index + lead).astype(jnp.bfloat16)
        lower = (chunk_index == row_index + lead + 1).astype(jnp.bfloat16)
        window = window.astype(jnp.bfloat16)
        beside = beside.astype(jnp.bfloat16)
        top = jnp.dot(upper, window, preferred_element_type=jnp.float32)
        top_beside = jnp.dot(upper, beside, preferred_element_type=jnp.float32)
        bottom = jnp.dot(lower, window, preferred_element_type=jnp.float32)
        bottom_beside = jnp.dot(lower, beside, preferred_element_type=jnp.float32)
        total = total + (
            gain_ref[member, layer_index, 0] * top
            + gain_ref[member, layer_index, 1] * top_beside
            + gain_ref[member, layer_index, 2] * bottom
            + gain_ref[member, layer_index, 3] * bottom_beside
        )
    phase_ref[0] = total


def trace_all(padded_rim, ray_shift, ray_weight, band_rows):
    layers, rim_rows, columns = padded_rim.shape
    members = ray_shift.shape[0]
    return pl.pallas_call(
        trace_kernel,
        out_shape=jax.ShapeDtypeStruct((members, band_rows, columns), jnp.float32),
        grid=(members,),
        in_specs=[
            pl.BlockSpec(memory_space=pltpu.SMEM),
            pl.BlockSpec(memory_space=pltpu.SMEM),
            pl.BlockSpec((layers, rim_rows, columns), lambda m: (0, 0, 0)),
        ],
        out_specs=pl.BlockSpec((1, band_rows, columns), lambda m: (m, 0, 0)),
        compiler_params=pltpu.CompilerParams(vmem_limit_bytes=48 * 1024 * 1024),
    )(ray_shift, ray_weight, padded_rim)


def windows(array, axis, count, stride, width):
    parts = [
        lax.slice_in_dim(array, offset, offset + stride * (count - 1) + 1, stride=stride, axis=axis)
        for offset in range(width)
    ]
    return jnp.stack(parts, axis=axis + 1)


def pack_symmetric(matrix):
    half = matrix.shape[0] // 2
    first, across, last = matrix[:half, :half], matrix[:half, half:], matrix[half:, half:]
    row = lax.broadcasted_iota(jnp.int32, (half, half + 1), 0)
    column = lax.broadcasted_iota(jnp.int32, (half, half + 1), 1)
    folded = jnp.where(
        column <= row, jnp.pad(last, ((0, 0), (0, 1))), jnp.pad(first, ((0, 0), (1, 0)))
    )
    return jnp.concatenate([folded.reshape(-1), across.reshape(-1)])


def unpack_symmetric(packed, extent):
    half = extent // 2
    folded = packed[: half * (half + 1)].reshape(half, half + 1)
    across = packed[half * (half + 1) :].reshape(half, half)
    row = lax.broadcasted_iota(jnp.int32, (half, half), 0)
    column = lax.broadcasted_iota(jnp.int32, (half, half), 1)
    last = jnp.where(column <= row, folded[:, :half], 0.0)
    first = jnp.where(column >= row, folded[:, 1:], 0.0)
    diagonal = (row == column).astype(jnp.float32)
    first = first + first.T * (1.0 - diagonal)
    last = last + last.T * (1.0 - diagonal)
    return jnp.concatenate(
        [jnp.concatenate([first, across], axis=1), jnp.concatenate([across.T, last], axis=1)],
        axis=0,
    )


def slot_gather(value, axes):
    for axis, size in axes:
        received = [
            lax.ppermute(value, axis, [(i, (i + offset) % size) for i in range(size)])
            for offset in range(1, size)
        ]
        for part in received:
            value = value + part
    return value


def on_device(screens, ray_shift, ray_weight, influence_index, influence, pupil_mask, petal):
    band_rows = screens.shape[1]
    padded_rim = band_stack_whole(screens)
    phases = trace_all(padded_rim, ray_shift, ray_weight, band_rows)
    tile_count = lax.axis_size("tile")
    dir_count = lax.axis_size("dir")
    direction_count = ray_shift.shape[0] * dir_count
    summed = jnp.sum(phases, axis=0)
    mean_phase = (
        lax.psum_scatter(
            summed.astype(jnp.bfloat16), "dir", scatter_dimension=1, tiled=True
        ).astype(jnp.float32)
        / direction_count
    )
    tiles_here = influence.shape[1]
    near_count = influence.shape[2]
    block_rows, block_columns = petal.shape
    ext_rows, ext_columns = block_rows + 2, block_columns + 2
    extent = ext_rows * ext_columns
    values = influence.astype(jnp.float32)
    onehot = (influence_index[..., None] == jnp.arange(extent, dtype=jnp.int32)).astype(
        jnp.float32
    )
    weights = pupil_mask.astype(jnp.float32).reshape(band_rows, tiles_here, 128)

    masked = (influence * weights[:, :, None, :].astype(jnp.bfloat16))
    gram = jnp.einsum(
        "rckp,rcjp->rckj", masked, influence, preferred_element_type=jnp.float32
    )
    placed = jnp.einsum("rckj,rcjb->rckb", gram, onehot, precision=highest)
    block_matrix = jnp.einsum("rcka,rckb->ab", onehot, placed, precision=highest)

    field = (weights * mean_phase.reshape(band_rows, tiles_here, 128))
    tile_terms = jnp.einsum("rckp,rcp->rck", values, field, precision=highest)
    block_rhs = jnp.einsum("rck,rcka->a", tile_terms, onehot, precision=highest)

    early = jnp.concatenate([pack_symmetric(block_matrix), petal.reshape(-1).astype(jnp.float32)])
    block_count = tile_count * dir_count
    slot = lax.axis_index("tile") * dir_count + lax.axis_index("dir")
    early = lax.psum(
        lax.dynamic_update_slice(
            jnp.zeros((block_count, early.shape[0]), jnp.float32), early[None], (slot, 0)
        ),
        ("tile", "dir"),
    )
    packed_count = extent * extent // 2 + extent // 2
    matrices = jax.vmap(lambda packed: unpack_symmetric(packed, extent))(early[:, :packed_count])
    petal_blocks = early[:, packed_count:].reshape(
        tile_count, dir_count, block_rows, block_columns
    )
    late = lax.dynamic_update_slice(
        jnp.zeros((block_count, extent), jnp.float32), block_rhs[None], (slot, 0)
    )
    rhs_blocks = slot_gather(late + 0.0 * early[0, 0], (("dir", dir_count), ("tile", tile_count)))
    grid_rows, grid_columns = tile_count * block_rows, dir_count * block_columns
    petal_grid = petal_blocks.transpose(0, 2, 1, 3).reshape(grid_rows, grid_columns)
    active = (petal_grid < 6).astype(jnp.float32)
    petals = (petal_grid[:, :, None] == jnp.arange(6, dtype=jnp.float32)).astype(jnp.float32)

    padded_rows, padded_columns = grid_rows + 2, grid_columns + 2
    row_pick = (
        lax.broadcasted_iota(jnp.int32, (tile_count, ext_rows, padded_rows), 2)
        == block_rows * lax.broadcasted_iota(jnp.int32, (tile_count, ext_rows, padded_rows), 0)
        + lax.broadcasted_iota(jnp.int32, (tile_count, ext_rows, padded_rows), 1)
    ).astype(jnp.float32).reshape(tile_count * ext_rows, padded_rows)
    column_pick = (
        lax.broadcasted_iota(jnp.int32, (padded_columns, dir_count, ext_columns), 0)
        == block_columns
        * lax.broadcasted_iota(jnp.int32, (padded_columns, dir_count, ext_columns), 1)
        + lax.broadcasted_iota(jnp.int32, (padded_columns, dir_count, ext_columns), 2)
    ).astype(jnp.float32).reshape(padded_columns, dir_count * ext_columns)

    def gather_blocks(padded):
        rows = jnp.dot(row_pick, padded, precision=highest)
        picked = jnp.dot(rows, column_pick, precision=highest)
        return (
            picked.reshape(tile_count, ext_rows, dir_count, ext_columns)
            .transpose(0, 2, 1, 3)
            .reshape(block_count, extent)
        )

    def spread_blocks(blocks):
        flat = (
            blocks.reshape(tile_count, dir_count, ext_rows, ext_columns)
            .transpose(0, 2, 1, 3)
            .reshape(tile_count * ext_rows, dir_count * ext_columns)
        )
        rows = jnp.dot(row_pick.T, flat, precision=highest)
        padded = jnp.dot(rows, column_pick.T, precision=highest)
        return padded[1:-1, 1:-1]

    def operator(vector):
        picked = gather_blocks(jnp.pad(vector, 1))
        terms = jnp.einsum("bij,bj->bi", matrices, picked, precision=highest)
        local_part = active * spread_blocks(terms) + ridge_weight * vector
        petal_totals = jnp.einsum("ijp,ij->p", petals, vector, precision=highest)
        return local_part + piston_weight * jnp.einsum(
            "ijp,p->ij", petals, petal_totals, precision=highest
        )

    rhs = active * spread_blocks(rhs_blocks)
    commands = jnp.zeros_like(rhs)
    residual = rhs
    direction = rhs
    norm_now = jnp.sum(residual * residual)
    for step_index in range(ITERS):
        applied = operator(direction)
        step_size = norm_now / jnp.sum(direction * applied)
        commands = commands + step_size * direction
        residual = residual - step_size * applied
        norm_next = jnp.sum(residual * residual)
        direction = residual + (norm_next / norm_now) * direction
        norm_now = norm_next

    row_at = lax.axis_index("tile") * block_rows
    column_at = lax.axis_index("dir") * block_columns
    own = lax.dynamic_slice(commands, (row_at, column_at), (block_rows, block_columns))
    extended = lax.dynamic_slice(
        jnp.pad(commands, 1), (row_at, column_at), (ext_rows, ext_columns)
    )
    picked = jnp.einsum("rcka,a->rck", onehot, extended.reshape(-1), precision=highest)
    fitted = jnp.einsum("rckp,rck->rcp", values, picked, precision=highest).reshape(
        band_rows, tiles_here * 128
    )
    whole_band = lax.all_gather(fitted.astype(jnp.bfloat16), "dir", axis=1, tiled=True).astype(
        fitted.dtype
    )
    corrected = (phases - whole_band[None]).astype(jnp.bfloat16)
    return (own, corrected)


def solution(mesh):
    in_specs = (
        P(None, "tile", None),
        P("dir", None, None),
        P("dir", None, None),
        P("tile", "dir", None),
        P("tile", "dir", None, None),
        P("tile", "dir"),
        P("tile", "dir"),
    )
    out_specs = (P("tile", "dir"), P("dir", "tile", None))
    return jax.shard_map(
        on_device, mesh=mesh, in_specs=in_specs, out_specs=out_specs, check_vma=False
    )
```

```python
import jax
import numpy as np
import jax.numpy as jnp
from jax import lax
from jax.experimental import pallas as pl
from jax.experimental.pallas import tpu as pltpu
from jax.sharding import PartitionSpec as P

SPAN = 2
AR_DEV = 3
AC_DEV = 12
ITERS = 3


ridge_weight = 1.0
piston_weight = 0.002
highest = lax.Precision.HIGHEST


def passed_along(array, axis, by):
    size = lax.axis_size(axis)
    return lax.ppermute(array, axis, [(i, (i + by) % size) for i in range(size)])


def band_stack_whole(piece):
    bands = []
    for offset in range(SPAN, -SPAN - 1, -1):
        if offset == 0:
            bands.append(piece)
        else:
            bands.append(passed_along(piece, "tile", offset))
    return jnp.concatenate(bands, axis=1)


def trace_kernel(shift_ref, gain_ref, rim_ref, phase_ref):
    member = pl.program_id(0)
    layers, rim_rows, columns = rim_ref.shape
    band_rows = phase_ref.shape[1]
    rim_depth = (rim_rows - band_rows) // 2
    chunk_rows = band_rows + 16
    total = jnp.zeros((band_rows, columns), jnp.float32)
    row_index = lax.broadcasted_iota(jnp.int32, (band_rows, chunk_rows), 0)
    chunk_index = lax.broadcasted_iota(jnp.int32, (band_rows, chunk_rows), 1)
    for layer_index in range(layers):
        first = rim_depth + shift_ref[member, layer_index, 0]
        start = jnp.clip((first // 16) * 16, 0, rim_rows - chunk_rows)
        start = pl.multiple_of(start, 16)
        lead = first - start
        chunk = rim_ref[layer_index, pl.ds(start, chunk_rows), :].astype(jnp.float32)
        turn = (columns - lax.rem(shift_ref[member, layer_index, 1], columns)) % columns
        window = pltpu.roll(chunk, turn, 1)
        beside = pltpu.roll(window, columns - 1, 1)
        upper = (chunk_index == row_index + lead).astype(jnp.bfloat16)
        lower = (chunk_index == row_index + lead + 1).astype(jnp.bfloat16)
        window = window.astype(jnp.bfloat16)
        beside = beside.astype(jnp.bfloat16)
        top = jnp.dot(upper, window, preferred_element_type=jnp.float32)
        top_beside = jnp.dot(upper, beside, preferred_element_type=jnp.float32)
        bottom = jnp.dot(lower, window, preferred_element_type=jnp.float32)
        bottom_beside = jnp.dot(lower, beside, preferred_element_type=jnp.float32)
        total = total + (
            gain_ref[member, layer_index, 0] * top
            + gain_ref[member, layer_index, 1] * top_beside
            + gain_ref[member, layer_index, 2] * bottom
            + gain_ref[member, layer_index, 3] * bottom_beside
        )
    phase_ref[0] = total


def trace_all(padded_rim, ray_shift, ray_weight, band_rows):
    layers, rim_rows, columns = padded_rim.shape
    members = ray_shift.shape[0]
    return pl.pallas_call(
        trace_kernel,
        out_shape=jax.ShapeDtypeStruct((members, band_rows, columns), jnp.float32),
        grid=(members,),
        in_specs=[
            pl.BlockSpec(memory_space=pltpu.SMEM),
            pl.BlockSpec(memory_space=pltpu.SMEM),
            pl.BlockSpec((layers, rim_rows, columns), lambda m: (0, 0, 0)),
        ],
        out_specs=pl.BlockSpec((1, band_rows, columns), lambda m: (m, 0, 0)),
        compiler_params=pltpu.CompilerParams(vmem_limit_bytes=48 * 1024 * 1024),
    )(ray_shift, ray_weight, padded_rim)


def windows(array, axis, count, stride, width):
    parts = [
        lax.slice_in_dim(array, offset, offset + stride * (count - 1) + 1, stride=stride, axis=axis)
        for offset in range(width)
    ]
    return jnp.stack(parts, axis=axis + 1)


def pack_symmetric(matrix):
    half = matrix.shape[0] // 2
    first, across, last = matrix[:half, :half], matrix[:half, half:], matrix[half:, half:]
    row = lax.broadcasted_iota(jnp.int32, (half, half + 1), 0)
    column = lax.broadcasted_iota(jnp.int32, (half, half + 1), 1)
    folded = jnp.where(
        column <= row, jnp.pad(last, ((0, 0), (0, 1))), jnp.pad(first, ((0, 0), (1, 0)))
    )
    return jnp.concatenate([folded.reshape(-1), across.reshape(-1)])


def unpack_symmetric(packed, extent):
    half = extent // 2
    folded = packed[: half * (half + 1)].reshape(half, half + 1)
    across = packed[half * (half + 1) :].reshape(half, half)
    row = lax.broadcasted_iota(jnp.int32, (half, half), 0)
    column = lax.broadcasted_iota(jnp.int32, (half, half), 1)
    last = jnp.where(column <= row, folded[:, :half], 0.0)
    first = jnp.where(column >= row, folded[:, 1:], 0.0)
    diagonal = (row == column).astype(jnp.float32)
    first = first + first.T * (1.0 - diagonal)
    last = last + last.T * (1.0 - diagonal)
    return jnp.concatenate(
        [jnp.concatenate([first, across], axis=1), jnp.concatenate([across.T, last], axis=1)],
        axis=0,
    )


def axis_gather(value, axis, size):
    parts = [value] + [
        lax.ppermute(value, axis, [(i, (i + offset) % size) for i in range(size)])
        for offset in range(1, size)
    ]
    order = (lax.axis_index(axis) - jnp.arange(size)) % size
    return jnp.take(jnp.stack(parts), order, axis=0)


def mesh_gather(value, tile_count, dir_count):
    gathered = axis_gather(axis_gather(value, "dir", dir_count), "tile", tile_count)
    return gathered.reshape((tile_count * dir_count,) + value.shape)


def on_device(screens, ray_shift, ray_weight, influence_index, influence, pupil_mask, petal):
    band_rows = screens.shape[1]
    padded_rim = band_stack_whole(screens)
    phases = trace_all(padded_rim, ray_shift, ray_weight, band_rows)
    tile_count = lax.axis_size("tile")
    dir_count = lax.axis_size("dir")
    direction_count = ray_shift.shape[0] * dir_count
    summed = jnp.sum(phases, axis=0)
    mean_phase = (
        lax.psum_scatter(
            summed.astype(jnp.bfloat16), "dir", scatter_dimension=1, tiled=True
        ).astype(jnp.float32)
        / direction_count
    )
    tiles_here = influence.shape[1]
    near_count = influence.shape[2]
    block_rows, block_columns = petal.shape
    ext_rows, ext_columns = block_rows + 2, block_columns + 2
    extent = ext_rows * ext_columns
    values = influence.astype(jnp.float32)
    onehot = (influence_index[..., None] == jnp.arange(extent, dtype=jnp.int32)).astype(
        jnp.float32
    )
    weights = pupil_mask.astype(jnp.float32).reshape(band_rows, tiles_here, 128)

    masked = (influence * weights[:, :, None, :].astype(jnp.bfloat16))
    gram = jnp.einsum(
        "rckp,rcjp->rckj", masked, influence, preferred_element_type=jnp.float32
    )
    placed = jnp.einsum("rckj,rcjb->rckb", gram, onehot, precision=highest)
    block_matrix = jnp.einsum("rcka,rckb->ab", onehot, placed, precision=highest)

    field = (weights * mean_phase.reshape(band_rows, tiles_here, 128))
    tile_terms = jnp.einsum("rckp,rcp->rck", values, field, precision=highest)
    block_rhs = jnp.einsum("rck,rcka->a", tile_terms, onehot, precision=highest)

    early = jnp.concatenate([pack_symmetric(block_matrix), petal.reshape(-1).astype(jnp.float32)])
    block_count = tile_count * dir_count
    early = mesh_gather(early, tile_count, dir_count)
    packed_count = extent * extent // 2 + extent // 2
    matrices = jax.vmap(lambda packed: unpack_symmetric(packed, extent))(early[:, :packed_count])
    petal_blocks = early[:, packed_count:].reshape(
        tile_count, dir_count, block_rows, block_columns
    )
    rhs_blocks = mesh_gather(block_rhs, tile_count, dir_count)
    grid_rows, grid_columns = tile_count * block_rows, dir_count * block_columns
    petal_grid = petal_blocks.transpose(0, 2, 1, 3).reshape(grid_rows, grid_columns)
    active = (petal_grid < 6).astype(jnp.float32)
    petals = (petal_grid[:, :, None] == jnp.arange(6, dtype=jnp.float32)).astype(jnp.float32)

    padded_rows, padded_columns = grid_rows + 2, grid_columns + 2
    row_pick = (
        lax.broadcasted_iota(jnp.int32, (tile_count, ext_rows, padded_rows), 2)
        == block_rows * lax.broadcasted_iota(jnp.int32, (tile_count, ext_rows, padded_rows), 0)
        + lax.broadcasted_iota(jnp.int32, (tile_count, ext_rows, padded_rows), 1)
    ).astype(jnp.float32).reshape(tile_count * ext_rows, padded_rows)
    column_pick = (
        lax.broadcasted_iota(jnp.int32, (padded_columns, dir_count, ext_columns), 0)
        == block_columns
        * lax.broadcasted_iota(jnp.int32, (padded_columns, dir_count, ext_columns), 1)
        + lax.broadcasted_iota(jnp.int32, (padded_columns, dir_count, ext_columns), 2)
    ).astype(jnp.float32).reshape(padded_columns, dir_count * ext_columns)

    def gather_blocks(padded):
        rows = jnp.dot(row_pick, padded, precision=highest)
        picked = jnp.dot(rows, column_pick, precision=highest)
        return (
            picked.reshape(tile_count, ext_rows, dir_count, ext_columns)
            .transpose(0, 2, 1, 3)
            .reshape(block_count, extent)
        )

    def spread_blocks(blocks):
        flat = (
            blocks.reshape(tile_count, dir_count, ext_rows, ext_columns)
            .transpose(0, 2, 1, 3)
            .reshape(tile_count * ext_rows, dir_count * ext_columns)
        )
        rows = jnp.dot(row_pick.T, flat, precision=highest)
        padded = jnp.dot(rows, column_pick.T, precision=highest)
        return padded[1:-1, 1:-1]

    def operator(vector):
        picked = gather_blocks(jnp.pad(vector, 1))
        terms = jnp.einsum("bij,bj->bi", matrices, picked, precision=highest)
        local_part = active * spread_blocks(terms) + ridge_weight * vector
        petal_totals = jnp.einsum("ijp,ij->p", petals, vector, precision=highest)
        return local_part + piston_weight * jnp.einsum(
            "ijp,p->ij", petals, petal_totals, precision=highest
        )

    rhs = active * spread_blocks(rhs_blocks)
    commands = jnp.zeros_like(rhs)
    residual = rhs
    direction = rhs
    norm_now = jnp.sum(residual * residual)
    for step_index in range(ITERS):
        applied = operator(direction)
        step_size = norm_now / jnp.sum(direction * applied)
        commands = commands + step_size * direction
        residual = residual - step_size * applied
        norm_next = jnp.sum(residual * residual)
        direction = residual + (norm_next / norm_now) * direction
        norm_now = norm_next

    row_at = lax.axis_index("tile") * block_rows
    column_at = lax.axis_index("dir") * block_columns
    own = lax.dynamic_slice(commands, (row_at, column_at), (block_rows, block_columns))
    extended = lax.dynamic_slice(
        jnp.pad(commands, 1), (row_at, column_at), (ext_rows, ext_columns)
    )
    picked = jnp.einsum("rcka,a->rck", onehot, extended.reshape(-1), precision=highest)
    fitted = jnp.einsum("rckp,rck->rcp", values, picked, precision=highest).reshape(
        band_rows, tiles_here * 128
    )
    whole_band = lax.all_gather(fitted.astype(jnp.bfloat16), "dir", axis=1, tiled=True).astype(
        fitted.dtype
    )
    corrected = (phases - whole_band[None]).astype(jnp.bfloat16)
    return (own, corrected)


def solution(mesh):
    in_specs = (
        P(None, "tile", None),
        P("dir", None, None),
        P("dir", None, None),
        P("tile", "dir", None),
        P("tile", "dir", None, None),
        P("tile", "dir"),
        P("tile", "dir"),
    )
    out_specs = (P("tile", "dir"), P("dir", "tile", None))
    return jax.shard_map(
        on_device, mesh=mesh, in_specs=in_specs, out_specs=out_specs, check_vma=False
    )
```

```python
import jax
import numpy as np
import jax.numpy as jnp
from jax import lax
from jax.experimental import pallas as pl
from jax.experimental.pallas import tpu as pltpu
from jax.sharding import PartitionSpec as P

SPAN = 2
AR_DEV = 3
AC_DEV = 12
ITERS = 3


ridge_weight = 1.0
piston_weight = 0.002
highest = lax.Precision.HIGHEST


def passed_along(array, axis, by):
    size = lax.axis_size(axis)
    return lax.ppermute(array, axis, [(i, (i + by) % size) for i in range(size)])


def band_stack_whole(piece):
    bands = []
    for offset in range(SPAN, -SPAN - 1, -1):
        if offset == 0:
            bands.append(piece)
        else:
            bands.append(passed_along(piece, "tile", offset))
    return jnp.concatenate(bands, axis=1)


def trace_kernel(shift_ref, gain_ref, rim_ref, phase_ref):
    member = pl.program_id(0)
    layers, rim_rows, columns = rim_ref.shape
    band_rows = phase_ref.shape[1]
    rim_depth = (rim_rows - band_rows) // 2
    chunk_rows = band_rows + 16
    total = jnp.zeros((band_rows, columns), jnp.float32)
    row_index = lax.broadcasted_iota(jnp.int32, (band_rows, chunk_rows), 0)
    chunk_index = lax.broadcasted_iota(jnp.int32, (band_rows, chunk_rows), 1)
    for layer_index in range(layers):
        first = rim_depth + shift_ref[member, layer_index, 0]
        start = jnp.clip((first // 16) * 16, 0, rim_rows - chunk_rows)
        start = pl.multiple_of(start, 16)
        lead = first - start
        chunk = rim_ref[layer_index, pl.ds(start, chunk_rows), :].astype(jnp.float32)
        turn = (columns - lax.rem(shift_ref[member, layer_index, 1], columns)) % columns
        window = pltpu.roll(chunk, turn, 1)
        beside = pltpu.roll(window, columns - 1, 1)
        upper = (chunk_index == row_index + lead).astype(jnp.bfloat16)
        lower = (chunk_index == row_index + lead + 1).astype(jnp.bfloat16)
        window = window.astype(jnp.bfloat16)
        beside = beside.astype(jnp.bfloat16)
        top = jnp.dot(upper, window, preferred_element_type=jnp.float32)
        top_beside = jnp.dot(upper, beside, preferred_element_type=jnp.float32)
        bottom = jnp.dot(lower, window, preferred_element_type=jnp.float32)
        bottom_beside = jnp.dot(lower, beside, preferred_element_type=jnp.float32)
        total = total + (
            gain_ref[member, layer_index, 0] * top
            + gain_ref[member, layer_index, 1] * top_beside
            + gain_ref[member, layer_index, 2] * bottom
            + gain_ref[member, layer_index, 3] * bottom_beside
        )
    phase_ref[0] = total


def trace_all(padded_rim, ray_shift, ray_weight, band_rows):
    layers, rim_rows, columns = padded_rim.shape
    members = ray_shift.shape[0]
    return pl.pallas_call(
        trace_kernel,
        out_shape=jax.ShapeDtypeStruct((members, band_rows, columns), jnp.float32),
        grid=(members,),
        in_specs=[
            pl.BlockSpec(memory_space=pltpu.SMEM),
            pl.BlockSpec(memory_space=pltpu.SMEM),
            pl.BlockSpec((layers, rim_rows, columns), lambda m: (0, 0, 0)),
        ],
        out_specs=pl.BlockSpec((1, band_rows, columns), lambda m: (m, 0, 0)),
        compiler_params=pltpu.CompilerParams(vmem_limit_bytes=48 * 1024 * 1024),
    )(ray_shift, ray_weight, padded_rim)


def windows(array, axis, count, stride, width):
    parts = [
        lax.slice_in_dim(array, offset, offset + stride * (count - 1) + 1, stride=stride, axis=axis)
        for offset in range(width)
    ]
    return jnp.stack(parts, axis=axis + 1)


def pack_symmetric(matrix):
    half = matrix.shape[0] // 2
    first, across, last = matrix[:half, :half], matrix[:half, half:], matrix[half:, half:]
    row = lax.broadcasted_iota(jnp.int32, (half, half + 1), 0)
    column = lax.broadcasted_iota(jnp.int32, (half, half + 1), 1)
    folded = jnp.where(
        column <= row, jnp.pad(last, ((0, 0), (0, 1))), jnp.pad(first, ((0, 0), (1, 0)))
    )
    return jnp.concatenate([folded.reshape(-1), across.reshape(-1)])


def unpack_symmetric(packed, extent):
    half = extent // 2
    folded = packed[: half * (half + 1)].reshape(half, half + 1)
    across = packed[half * (half + 1) :].reshape(half, half)
    row = lax.broadcasted_iota(jnp.int32, (half, half), 0)
    column = lax.broadcasted_iota(jnp.int32, (half, half), 1)
    last = jnp.where(column <= row, folded[:, :half], 0.0)
    first = jnp.where(column >= row, folded[:, 1:], 0.0)
    diagonal = (row == column).astype(jnp.float32)
    first = first + first.T * (1.0 - diagonal)
    last = last + last.T * (1.0 - diagonal)
    return jnp.concatenate(
        [jnp.concatenate([first, across], axis=1), jnp.concatenate([across.T, last], axis=1)],
        axis=0,
    )


def axis_gather(value, axis, size):
    parts = [value] + [
        lax.ppermute(value, axis, [(i, (i + offset) % size) for i in range(size)])
        for offset in range(1, size)
    ]
    order = (lax.axis_index(axis) - jnp.arange(size)) % size
    return jnp.take(jnp.stack(parts), order, axis=0)


def mesh_gather(value, tile_count, dir_count):
    gathered = axis_gather(axis_gather(value, "dir", dir_count), "tile", tile_count)
    return gathered.reshape((tile_count * dir_count,) + value.shape)


def on_device(screens, ray_shift, ray_weight, influence_index, influence, pupil_mask, petal):
    band_rows = screens.shape[1]
    padded_rim = band_stack_whole(screens)
    arrived = jnp.sum(padded_rim[:, ::band_rows, :1].astype(jnp.float32))
    phases = trace_all(padded_rim, ray_shift, ray_weight, band_rows)
    tile_count = lax.axis_size("tile")
    dir_count = lax.axis_size("dir")
    direction_count = ray_shift.shape[0] * dir_count
    summed = jnp.sum(phases, axis=0)
    block_width = summed.shape[1] // dir_count
    by_block = summed.reshape(band_rows, dir_count, block_width).transpose(1, 0, 2)
    own_column = lax.axis_index("dir")
    column_sum = jnp.take(by_block, own_column, axis=0)
    for offset in range(1, dir_count):
        outgoing = jnp.take(by_block, (own_column + offset) % dir_count, axis=0)
        column_sum = column_sum + lax.ppermute(
            outgoing, "dir", [(i, (i + offset) % dir_count) for i in range(dir_count)]
        )
    mean_phase = column_sum / direction_count
    tiles_here = influence.shape[1]
    near_count = influence.shape[2]
    block_rows, block_columns = petal.shape
    ext_rows, ext_columns = block_rows + 2, block_columns + 2
    extent = ext_rows * ext_columns
    values = influence.astype(jnp.float32)
    onehot = (influence_index[..., None] == jnp.arange(extent, dtype=jnp.int32)).astype(
        jnp.float32
    )
    weights = pupil_mask.astype(jnp.float32).reshape(band_rows, tiles_here, 128)

    masked = (influence * weights[:, :, None, :].astype(jnp.bfloat16))
    gram = jnp.einsum(
        "rckp,rcjp->rckj", masked, influence, preferred_element_type=jnp.float32
    )
    placed = jnp.einsum("rckj,rcjb->rckb", gram, onehot, precision=highest)
    block_matrix = jnp.einsum("rcka,rckb->ab", onehot, placed, precision=highest)

    field = (weights * mean_phase.reshape(band_rows, tiles_here, 128))
    tile_terms = jnp.einsum("rckp,rcp->rck", values, field, precision=highest)
    block_rhs = jnp.einsum("rck,rcka->a", tile_terms, onehot, precision=highest)

    early = jnp.concatenate([pack_symmetric(block_matrix), petal.reshape(-1).astype(jnp.float32)])
    block_count = tile_count * dir_count
    early = mesh_gather(early + 0.0 * arrived, tile_count, dir_count)
    packed_count = extent * extent // 2 + extent // 2
    matrices = jax.vmap(lambda packed: unpack_symmetric(packed, extent))(early[:, :packed_count])
    petal_blocks = early[:, packed_count:].reshape(
        tile_count, dir_count, block_rows, block_columns
    )
    rhs_blocks = mesh_gather(block_rhs, tile_count, dir_count)
    grid_rows, grid_columns = tile_count * block_rows, dir_count * block_columns
    petal_grid = petal_blocks.transpose(0, 2, 1, 3).reshape(grid_rows, grid_columns)
    active = (petal_grid < 6).astype(jnp.float32)
    petals = (petal_grid[:, :, None] == jnp.arange(6, dtype=jnp.float32)).astype(jnp.float32)

    padded_rows, padded_columns = grid_rows + 2, grid_columns + 2
    row_pick = (
        lax.broadcasted_iota(jnp.int32, (tile_count, ext_rows, padded_rows), 2)
        == block_rows * lax.broadcasted_iota(jnp.int32, (tile_count, ext_rows, padded_rows), 0)
        + lax.broadcasted_iota(jnp.int32, (tile_count, ext_rows, padded_rows), 1)
    ).astype(jnp.float32).reshape(tile_count * ext_rows, padded_rows)
    column_pick = (
        lax.broadcasted_iota(jnp.int32, (padded_columns, dir_count, ext_columns), 0)
        == block_columns
        * lax.broadcasted_iota(jnp.int32, (padded_columns, dir_count, ext_columns), 1)
        + lax.broadcasted_iota(jnp.int32, (padded_columns, dir_count, ext_columns), 2)
    ).astype(jnp.float32).reshape(padded_columns, dir_count * ext_columns)

    def gather_blocks(padded):
        rows = jnp.dot(row_pick, padded, precision=highest)
        picked = jnp.dot(rows, column_pick, precision=highest)
        return (
            picked.reshape(tile_count, ext_rows, dir_count, ext_columns)
            .transpose(0, 2, 1, 3)
            .reshape(block_count, extent)
        )

    def spread_blocks(blocks):
        flat = (
            blocks.reshape(tile_count, dir_count, ext_rows, ext_columns)
            .transpose(0, 2, 1, 3)
            .reshape(tile_count * ext_rows, dir_count * ext_columns)
        )
        rows = jnp.dot(row_pick.T, flat, precision=highest)
        padded = jnp.dot(rows, column_pick.T, precision=highest)
        return padded[1:-1, 1:-1]

    def operator(vector):
        picked = gather_blocks(jnp.pad(vector, 1))
        terms = jnp.einsum("bij,bj->bi", matrices, picked, precision=highest)
        local_part = active * spread_blocks(terms) + ridge_weight * vector
        petal_totals = jnp.einsum("ijp,ij->p", petals, vector, precision=highest)
        return local_part + piston_weight * jnp.einsum(
            "ijp,p->ij", petals, petal_totals, precision=highest
        )

    rhs = active * spread_blocks(rhs_blocks)
    commands = jnp.zeros_like(rhs)
    residual = rhs
    direction = rhs
    norm_now = jnp.sum(residual * residual)
    for step_index in range(ITERS):
        applied = operator(direction)
        step_size = norm_now / jnp.sum(direction * applied)
        commands = commands + step_size * direction
        residual = residual - step_size * applied
        norm_next = jnp.sum(residual * residual)
        direction = residual + (norm_next / norm_now) * direction
        norm_now = norm_next

    row_at = lax.axis_index("tile") * block_rows
    column_at = lax.axis_index("dir") * block_columns
    own = lax.dynamic_slice(commands, (row_at, column_at), (block_rows, block_columns))
    extended = lax.dynamic_slice(
        jnp.pad(commands, 1), (row_at, column_at), (ext_rows, ext_columns)
    )
    picked = jnp.einsum("rcka,a->rck", onehot, extended.reshape(-1), precision=highest)
    fitted = jnp.einsum("rckp,rck->rcp", values, picked, precision=highest).reshape(
        band_rows, tiles_here * 128
    )
    whole_band = (
        axis_gather(fitted.astype(jnp.bfloat16), "dir", dir_count)
        .transpose(1, 0, 2)
        .reshape(band_rows, dir_count * fitted.shape[1])
        .astype(fitted.dtype)
    )
    corrected = (phases - whole_band[None]).astype(jnp.bfloat16)
    return (own, corrected)


def solution(mesh):
    in_specs = (
        P(None, "tile", None),
        P("dir", None, None),
        P("dir", None, None),
        P("tile", "dir", None),
        P("tile", "dir", None, None),
        P("tile", "dir"),
        P("tile", "dir"),
    )
    out_specs = (P("tile", "dir"), P("dir", "tile", None))
    return jax.shard_map(
        on_device, mesh=mesh, in_specs=in_specs, out_specs=out_specs, check_vma=False
    )
```

```python
import jax
import numpy as np
import jax.numpy as jnp
from jax import lax
from jax.experimental import pallas as pl
from jax.experimental.pallas import tpu as pltpu
from jax.sharding import PartitionSpec as P

SPAN = 2
AR_DEV = 3
AC_DEV = 12
ITERS = 3


ridge_weight = 1.0
piston_weight = 0.002
highest = lax.Precision.HIGHEST


def passed_along(array, axis, by):
    size = lax.axis_size(axis)
    return lax.ppermute(array, axis, [(i, (i + by) % size) for i in range(size)])


def band_stack_whole(piece):
    bands = []
    for offset in range(SPAN, -SPAN - 1, -1):
        if offset == 0:
            bands.append(piece)
        else:
            bands.append(passed_along(piece, "tile", offset))
    return jnp.concatenate(bands, axis=1)


def trace_kernel(shift_ref, gain_ref, rim_ref, phase_ref):
    member = pl.program_id(0)
    layers, rim_rows, columns = rim_ref.shape
    band_rows = phase_ref.shape[1]
    rim_depth = (rim_rows - band_rows) // 2
    chunk_rows = band_rows + 16
    total = jnp.zeros((band_rows, columns), jnp.float32)
    row_index = lax.broadcasted_iota(jnp.int32, (band_rows, chunk_rows), 0)
    chunk_index = lax.broadcasted_iota(jnp.int32, (band_rows, chunk_rows), 1)
    for layer_index in range(layers):
        first = rim_depth + shift_ref[member, layer_index, 0]
        start = jnp.clip((first // 16) * 16, 0, rim_rows - chunk_rows)
        start = pl.multiple_of(start, 16)
        lead = first - start
        chunk = rim_ref[layer_index, pl.ds(start, chunk_rows), :].astype(jnp.float32)
        turn = (columns - lax.rem(shift_ref[member, layer_index, 1], columns)) % columns
        window = pltpu.roll(chunk, turn, 1)
        beside = pltpu.roll(window, columns - 1, 1)
        upper = (chunk_index == row_index + lead).astype(jnp.bfloat16)
        lower = (chunk_index == row_index + lead + 1).astype(jnp.bfloat16)
        window = window.astype(jnp.bfloat16)
        beside = beside.astype(jnp.bfloat16)
        top = jnp.dot(upper, window, preferred_element_type=jnp.float32)
        top_beside = jnp.dot(upper, beside, preferred_element_type=jnp.float32)
        bottom = jnp.dot(lower, window, preferred_element_type=jnp.float32)
        bottom_beside = jnp.dot(lower, beside, preferred_element_type=jnp.float32)
        total = total + (
            gain_ref[member, layer_index, 0] * top
            + gain_ref[member, layer_index, 1] * top_beside
            + gain_ref[member, layer_index, 2] * bottom
            + gain_ref[member, layer_index, 3] * bottom_beside
        )
    phase_ref[0] = total


def trace_all(padded_rim, ray_shift, ray_weight, band_rows):
    layers, rim_rows, columns = padded_rim.shape
    members = ray_shift.shape[0]
    return pl.pallas_call(
        trace_kernel,
        out_shape=jax.ShapeDtypeStruct((members, band_rows, columns), jnp.float32),
        grid=(members,),
        in_specs=[
            pl.BlockSpec(memory_space=pltpu.SMEM),
            pl.BlockSpec(memory_space=pltpu.SMEM),
            pl.BlockSpec((layers, rim_rows, columns), lambda m: (0, 0, 0)),
        ],
        out_specs=pl.BlockSpec((1, band_rows, columns), lambda m: (m, 0, 0)),
        compiler_params=pltpu.CompilerParams(vmem_limit_bytes=48 * 1024 * 1024),
    )(ray_shift, ray_weight, padded_rim)


def windows(array, axis, count, stride, width):
    parts = [
        lax.slice_in_dim(array, offset, offset + stride * (count - 1) + 1, stride=stride, axis=axis)
        for offset in range(width)
    ]
    return jnp.stack(parts, axis=axis + 1)


def axis_gather(value, axis, size):
    parts = [value] + [
        lax.ppermute(value, axis, [(i, (i + offset) % size) for i in range(size)])
        for offset in range(1, size)
    ]
    order = (lax.axis_index(axis) - jnp.arange(size)) % size
    return jnp.take(jnp.stack(parts), order, axis=0)


def mesh_gather(value, tile_count, dir_count):
    gathered = axis_gather(axis_gather(value, "dir", dir_count), "tile", tile_count)
    return gathered.reshape((tile_count * dir_count,) + value.shape)


def on_device(screens, ray_shift, ray_weight, influence_index, influence, pupil_mask, petal):
    band_rows = screens.shape[1]
    padded_rim = band_stack_whole(screens)
    arrived = jnp.sum(padded_rim[:, ::band_rows, :1].astype(jnp.float32))
    phases = trace_all(padded_rim, ray_shift, ray_weight, band_rows)
    tile_count = lax.axis_size("tile")
    dir_count = lax.axis_size("dir")
    direction_count = ray_shift.shape[0] * dir_count
    summed = jnp.sum(phases, axis=0)
    block_width = summed.shape[1] // dir_count
    by_block = summed.reshape(band_rows, dir_count, block_width).transpose(1, 0, 2)
    own_column = lax.axis_index("dir")
    column_sum = jnp.take(by_block, own_column, axis=0)
    for offset in range(1, dir_count):
        outgoing = jnp.take(by_block, (own_column + offset) % dir_count, axis=0)
        column_sum = column_sum + lax.ppermute(
            outgoing, "dir", [(i, (i + offset) % dir_count) for i in range(dir_count)]
        )
    mean_phase = column_sum / direction_count
    tiles_here = influence.shape[1]
    near_count = influence.shape[2]
    block_rows, block_columns = petal.shape
    ext_rows, ext_columns = block_rows + 2, block_columns + 2
    extent = ext_rows * ext_columns
    values = influence.astype(jnp.float32)
    onehot = (influence_index[..., None] == jnp.arange(extent, dtype=jnp.int32)).astype(
        jnp.float32
    )
    weights = pupil_mask.astype(jnp.float32).reshape(band_rows, tiles_here, 128)

    masked = (influence * weights[:, :, None, :].astype(jnp.bfloat16))
    gram = jnp.einsum(
        "rckp,rcjp->rckj", masked, influence, preferred_element_type=jnp.float32
    )
    placed = jnp.einsum("rckj,rcjb->rckb", gram, onehot, precision=highest)
    block_matrix = jnp.einsum("rcka,rckb->ab", onehot, placed, precision=highest)

    field = (weights * mean_phase.reshape(band_rows, tiles_here, 128))
    tile_terms = jnp.einsum("rckp,rcp->rck", values, field, precision=highest)
    block_rhs = jnp.einsum("rck,rcka->a", tile_terms, onehot, precision=highest)

    half = extent // 2
    petal_row = jnp.pad(
        petal.reshape(1, -1).astype(jnp.float32), ((0, 0), (0, 3 * half - petal.size))
    )
    early = jnp.concatenate(
        [
            jnp.concatenate(
                [block_matrix[:half, :half], block_matrix[:half, half:], block_matrix[half:, half:]],
                axis=1,
            ),
            petal_row,
        ],
        axis=0,
    )
    block_count = tile_count * dir_count
    early = mesh_gather(early + 0.0 * arrived, tile_count, dir_count)
    first_part = early[:, :half, :half]
    across_part = early[:, :half, half : 2 * half]
    last_part = early[:, :half, 2 * half :]
    petal_blocks = early[:, half, : petal.size].reshape(
        tile_count, dir_count, block_rows, block_columns
    )
    rhs_blocks = mesh_gather(block_rhs, tile_count, dir_count)
    grid_rows, grid_columns = tile_count * block_rows, dir_count * block_columns
    petal_grid = petal_blocks.transpose(0, 2, 1, 3).reshape(grid_rows, grid_columns)
    active = (petal_grid < 6).astype(jnp.float32)
    petals = (petal_grid[:, :, None] == jnp.arange(6, dtype=jnp.float32)).astype(jnp.float32)

    padded_rows, padded_columns = grid_rows + 2, grid_columns + 2
    row_pick = (
        lax.broadcasted_iota(jnp.int32, (tile_count, ext_rows, padded_rows), 2)
        == block_rows * lax.broadcasted_iota(jnp.int32, (tile_count, ext_rows, padded_rows), 0)
        + lax.broadcasted_iota(jnp.int32, (tile_count, ext_rows, padded_rows), 1)
    ).astype(jnp.float32).reshape(tile_count * ext_rows, padded_rows)
    column_pick = (
        lax.broadcasted_iota(jnp.int32, (padded_columns, dir_count, ext_columns), 0)
        == block_columns
        * lax.broadcasted_iota(jnp.int32, (padded_columns, dir_count, ext_columns), 1)
        + lax.broadcasted_iota(jnp.int32, (padded_columns, dir_count, ext_columns), 2)
    ).astype(jnp.float32).reshape(padded_columns, dir_count * ext_columns)

    def gather_blocks(padded):
        rows = jnp.dot(row_pick, padded, precision=highest)
        picked = jnp.dot(rows, column_pick, precision=highest)
        return (
            picked.reshape(tile_count, ext_rows, dir_count, ext_columns)
            .transpose(0, 2, 1, 3)
            .reshape(block_count, extent)
        )

    def spread_blocks(blocks):
        flat = (
            blocks.reshape(tile_count, dir_count, ext_rows, ext_columns)
            .transpose(0, 2, 1, 3)
            .reshape(tile_count * ext_rows, dir_count * ext_columns)
        )
        rows = jnp.dot(row_pick.T, flat, precision=highest)
        padded = jnp.dot(rows, column_pick.T, precision=highest)
        return padded[1:-1, 1:-1]

    def operator(vector):
        picked = gather_blocks(jnp.pad(vector, 1))
        head, tail = picked[:, :half], picked[:, half:]
        terms = jnp.concatenate(
            [
                jnp.einsum("bij,bj->bi", first_part, head, precision=highest)
                + jnp.einsum("bij,bj->bi", across_part, tail, precision=highest),
                jnp.einsum("bji,bj->bi", across_part, head, precision=highest)
                + jnp.einsum("bij,bj->bi", last_part, tail, precision=highest),
            ],
            axis=1,
        )
        local_part = active * spread_blocks(terms) + ridge_weight * vector
        petal_totals = jnp.einsum("ijp,ij->p", petals, vector, precision=highest)
        return local_part + piston_weight * jnp.einsum(
            "ijp,p->ij", petals, petal_totals, precision=highest
        )

    rhs = active * spread_blocks(rhs_blocks)
    commands = jnp.zeros_like(rhs)
    residual = rhs
    direction = rhs
    norm_now = jnp.sum(residual * residual)
    for step_index in range(ITERS):
        applied = operator(direction)
        step_size = norm_now / jnp.sum(direction * applied)
        commands = commands + step_size * direction
        residual = residual - step_size * applied
        norm_next = jnp.sum(residual * residual)
        direction = residual + (norm_next / norm_now) * direction
        norm_now = norm_next

    row_at = lax.axis_index("tile") * block_rows
    column_at = lax.axis_index("dir") * block_columns
    own = lax.dynamic_slice(commands, (row_at, column_at), (block_rows, block_columns))
    extended = lax.dynamic_slice(
        jnp.pad(commands, 1), (row_at, column_at), (ext_rows, ext_columns)
    )
    picked = jnp.einsum("rcka,a->rck", onehot, extended.reshape(-1), precision=highest)
    fitted = jnp.einsum("rckp,rck->rcp", values, picked, precision=highest).reshape(
        band_rows, tiles_here * 128
    )
    whole_band = (
        axis_gather(fitted.astype(jnp.bfloat16), "dir", dir_count)
        .transpose(1, 0, 2)
        .reshape(band_rows, dir_count * fitted.shape[1])
        .astype(fitted.dtype)
    )
    corrected = (phases - whole_band[None]).astype(jnp.bfloat16)
    return (own, corrected)


def solution(mesh):
    in_specs = (
        P(None, "tile", None),
        P("dir", None, None),
        P("dir", None, None),
        P("tile", "dir", None),
        P("tile", "dir", None, None),
        P("tile", "dir"),
        P("tile", "dir"),
    )
    out_specs = (P("tile", "dir"), P("dir", "tile", None))
    return jax.shard_map(
        on_device, mesh=mesh, in_specs=in_specs, out_specs=out_specs, check_vma=False
    )
```

```python
import jax
import numpy as np
import jax.numpy as jnp
from jax import lax
from jax.experimental import pallas as pl
from jax.experimental.pallas import tpu as pltpu
from jax.sharding import PartitionSpec as P

SPAN = 2
AR_DEV = 3
AC_DEV = 12
ITERS = 3


ridge_weight = 1.0
piston_weight = 0.002
highest = lax.Precision.HIGHEST


def passed_along(array, axis, by):
    size = lax.axis_size(axis)
    return lax.ppermute(array, axis, [(i, (i + by) % size) for i in range(size)])


def band_stack_whole(piece):
    size = lax.axis_size("tile")
    partner = [(i, i ^ 1) for i in range(size)]
    from_below = passed_along(piece, "tile", 2)
    from_above = passed_along(piece, "tile", -2)
    beside = lax.ppermute(piece, "tile", partner)
    second = lax.axis_index("tile") % 2 == 1
    relayed = lax.ppermute(jnp.where(second, from_below, from_above), "tile", partner)
    lower = jnp.where(second, beside, relayed)
    upper = jnp.where(second, relayed, beside)
    return jnp.concatenate([from_below, lower, piece, upper, from_above], axis=1)


def trace_kernel(shift_ref, gain_ref, rim_ref, phase_ref):
    member = pl.program_id(0)
    layers, rim_rows, columns = rim_ref.shape
    band_rows = phase_ref.shape[1]
    rim_depth = (rim_rows - band_rows) // 2
    chunk_rows = band_rows + 16
    total = jnp.zeros((band_rows, columns), jnp.float32)
    row_index = lax.broadcasted_iota(jnp.int32, (band_rows, chunk_rows), 0)
    chunk_index = lax.broadcasted_iota(jnp.int32, (band_rows, chunk_rows), 1)
    for layer_index in range(layers):
        first = rim_depth + shift_ref[member, layer_index, 0]
        start = jnp.clip((first // 16) * 16, 0, rim_rows - chunk_rows)
        start = pl.multiple_of(start, 16)
        lead = first - start
        chunk = rim_ref[layer_index, pl.ds(start, chunk_rows), :].astype(jnp.float32)
        turn = (columns - lax.rem(shift_ref[member, layer_index, 1], columns)) % columns
        window = pltpu.roll(chunk, turn, 1)
        beside = pltpu.roll(window, columns - 1, 1)
        upper = (chunk_index == row_index + lead).astype(jnp.bfloat16)
        lower = (chunk_index == row_index + lead + 1).astype(jnp.bfloat16)
        window = window.astype(jnp.bfloat16)
        beside = beside.astype(jnp.bfloat16)
        top = jnp.dot(upper, window, preferred_element_type=jnp.float32)
        top_beside = jnp.dot(upper, beside, preferred_element_type=jnp.float32)
        bottom = jnp.dot(lower, window, preferred_element_type=jnp.float32)
        bottom_beside = jnp.dot(lower, beside, preferred_element_type=jnp.float32)
        total = total + (
            gain_ref[member, layer_index, 0] * top
            + gain_ref[member, layer_index, 1] * top_beside
            + gain_ref[member, layer_index, 2] * bottom
            + gain_ref[member, layer_index, 3] * bottom_beside
        )
    phase_ref[0] = total


def trace_all(padded_rim, ray_shift, ray_weight, band_rows):
    layers, rim_rows, columns = padded_rim.shape
    members = ray_shift.shape[0]
    return pl.pallas_call(
        trace_kernel,
        out_shape=jax.ShapeDtypeStruct((members, band_rows, columns), jnp.float32),
        grid=(members,),
        in_specs=[
            pl.BlockSpec(memory_space=pltpu.SMEM),
            pl.BlockSpec(memory_space=pltpu.SMEM),
            pl.BlockSpec((layers, rim_rows, columns), lambda m: (0, 0, 0)),
        ],
        out_specs=pl.BlockSpec((1, band_rows, columns), lambda m: (m, 0, 0)),
        compiler_params=pltpu.CompilerParams(vmem_limit_bytes=48 * 1024 * 1024),
    )(ray_shift, ray_weight, padded_rim)


def windows(array, axis, count, stride, width):
    parts = [
        lax.slice_in_dim(array, offset, offset + stride * (count - 1) + 1, stride=stride, axis=axis)
        for offset in range(width)
    ]
    return jnp.stack(parts, axis=axis + 1)


def axis_gather(value, axis, size):
    parts = [value] + [
        lax.ppermute(value, axis, [(i, (i + offset) % size) for i in range(size)])
        for offset in range(1, size)
    ]
    order = (lax.axis_index(axis) - jnp.arange(size)) % size
    return jnp.take(jnp.stack(parts), order, axis=0)


def mesh_gather(value, tile_count, dir_count):
    gathered = axis_gather(axis_gather(value, "dir", dir_count), "tile", tile_count)
    return gathered.reshape((tile_count * dir_count,) + value.shape)


def on_device(screens, ray_shift, ray_weight, influence_index, influence, pupil_mask, petal):
    band_rows = screens.shape[1]
    padded_rim = band_stack_whole(screens)
    arrived = jnp.sum(padded_rim[:, ::band_rows, :1].astype(jnp.float32))
    phases = trace_all(padded_rim, ray_shift, ray_weight, band_rows)
    tile_count = lax.axis_size("tile")
    dir_count = lax.axis_size("dir")
    direction_count = ray_shift.shape[0] * dir_count
    summed = jnp.sum(phases, axis=0)
    block_width = summed.shape[1] // dir_count
    by_block = summed.reshape(band_rows, dir_count, block_width).transpose(1, 0, 2)
    own_column = lax.axis_index("dir")
    column_sum = jnp.take(by_block, own_column, axis=0)
    for offset in range(1, dir_count):
        outgoing = jnp.take(by_block, (own_column + offset) % dir_count, axis=0)
        column_sum = column_sum + lax.ppermute(
            outgoing, "dir", [(i, (i + offset) % dir_count) for i in range(dir_count)]
        )
    mean_phase = column_sum / direction_count
    tiles_here = influence.shape[1]
    near_count = influence.shape[2]
    block_rows, block_columns = petal.shape
    ext_rows, ext_columns = block_rows + 2, block_columns + 2
    extent = ext_rows * ext_columns
    values = influence.astype(jnp.float32)
    onehot = (influence_index[..., None] == jnp.arange(extent, dtype=jnp.int32)).astype(
        jnp.float32
    )
    weights = pupil_mask.astype(jnp.float32).reshape(band_rows, tiles_here, 128)

    masked = (influence * weights[:, :, None, :].astype(jnp.bfloat16))
    gram = jnp.einsum(
        "rckp,rcjp->rckj", masked, influence, preferred_element_type=jnp.float32
    )
    placed = jnp.einsum("rckj,rcjb->rckb", gram, onehot, precision=highest)
    block_matrix = jnp.einsum("rcka,rckb->ab", onehot, placed, precision=highest)

    field = (weights * mean_phase.reshape(band_rows, tiles_here, 128))
    tile_terms = jnp.einsum("rckp,rcp->rck", values, field, precision=highest)
    block_rhs = jnp.einsum("rck,rcka->a", tile_terms, onehot, precision=highest)

    half = extent // 2
    petal_row = jnp.pad(
        petal.reshape(1, -1).astype(jnp.float32), ((0, 0), (0, 3 * half - petal.size))
    )
    early = jnp.concatenate(
        [
            jnp.concatenate(
                [block_matrix[:half, :half], block_matrix[:half, half:], block_matrix[half:, half:]],
                axis=1,
            ),
            petal_row,
        ],
        axis=0,
    )
    block_count = tile_count * dir_count
    early = mesh_gather(early + 0.0 * arrived, tile_count, dir_count)
    first_part = early[:, :half, :half]
    across_part = early[:, :half, half : 2 * half]
    last_part = early[:, :half, 2 * half :]
    petal_blocks = early[:, half, : petal.size].reshape(
        tile_count, dir_count, block_rows, block_columns
    )
    rhs_blocks = mesh_gather(block_rhs, tile_count, dir_count)
    grid_rows, grid_columns = tile_count * block_rows, dir_count * block_columns
    petal_grid = petal_blocks.transpose(0, 2, 1, 3).reshape(grid_rows, grid_columns)
    active = (petal_grid < 6).astype(jnp.float32)
    petals = (petal_grid[:, :, None] == jnp.arange(6, dtype=jnp.float32)).astype(jnp.float32)

    padded_rows, padded_columns = grid_rows + 2, grid_columns + 2
    row_pick = (
        lax.broadcasted_iota(jnp.int32, (tile_count, ext_rows, padded_rows), 2)
        == block_rows * lax.broadcasted_iota(jnp.int32, (tile_count, ext_rows, padded_rows), 0)
        + lax.broadcasted_iota(jnp.int32, (tile_count, ext_rows, padded_rows), 1)
    ).astype(jnp.float32).reshape(tile_count * ext_rows, padded_rows)
    column_pick = (
        lax.broadcasted_iota(jnp.int32, (padded_columns, dir_count, ext_columns), 0)
        == block_columns
        * lax.broadcasted_iota(jnp.int32, (padded_columns, dir_count, ext_columns), 1)
        + lax.broadcasted_iota(jnp.int32, (padded_columns, dir_count, ext_columns), 2)
    ).astype(jnp.float32).reshape(padded_columns, dir_count * ext_columns)

    def gather_blocks(padded):
        rows = jnp.dot(row_pick, padded, precision=highest)
        picked = jnp.dot(rows, column_pick, precision=highest)
        return (
            picked.reshape(tile_count, ext_rows, dir_count, ext_columns)
            .transpose(0, 2, 1, 3)
            .reshape(block_count, extent)
        )

    def spread_blocks(blocks):
        flat = (
            blocks.reshape(tile_count, dir_count, ext_rows, ext_columns)
            .transpose(0, 2, 1, 3)
            .reshape(tile_count * ext_rows, dir_count * ext_columns)
        )
        rows = jnp.dot(row_pick.T, flat, precision=highest)
        padded = jnp.dot(rows, column_pick.T, precision=highest)
        return padded[1:-1, 1:-1]

    def operator(vector):
        picked = gather_blocks(jnp.pad(vector, 1))
        head, tail = picked[:, :half], picked[:, half:]
        terms = jnp.concatenate(
            [
                jnp.einsum("bij,bj->bi", first_part, head, precision=highest)
                + jnp.einsum("bij,bj->bi", across_part, tail, precision=highest),
                jnp.einsum("bji,bj->bi", across_part, head, precision=highest)
                + jnp.einsum("bij,bj->bi", last_part, tail, precision=highest),
            ],
            axis=1,
        )
        local_part = active * spread_blocks(terms) + ridge_weight * vector
        petal_totals = jnp.einsum("ijp,ij->p", petals, vector, precision=highest)
        return local_part + piston_weight * jnp.einsum(
            "ijp,p->ij", petals, petal_totals, precision=highest
        )

    rhs = active * spread_blocks(rhs_blocks)
    commands = jnp.zeros_like(rhs)
    residual = rhs
    direction = rhs
    norm_now = jnp.sum(residual * residual)
    for step_index in range(ITERS):
        applied = operator(direction)
        step_size = norm_now / jnp.sum(direction * applied)
        commands = commands + step_size * direction
        residual = residual - step_size * applied
        norm_next = jnp.sum(residual * residual)
        direction = residual + (norm_next / norm_now) * direction
        norm_now = norm_next

    row_at = lax.axis_index("tile") * block_rows
    column_at = lax.axis_index("dir") * block_columns
    own = lax.dynamic_slice(commands, (row_at, column_at), (block_rows, block_columns))
    extended = lax.dynamic_slice(
        jnp.pad(commands, 1), (row_at, column_at), (ext_rows, ext_columns)
    )
    picked = jnp.einsum("rcka,a->rck", onehot, extended.reshape(-1), precision=highest)
    fitted = jnp.einsum("rckp,rck->rcp", values, picked, precision=highest).reshape(
        band_rows, tiles_here * 128
    )
    whole_band = (
        axis_gather(fitted.astype(jnp.bfloat16), "dir", dir_count)
        .transpose(1, 0, 2)
        .reshape(band_rows, dir_count * fitted.shape[1])
        .astype(fitted.dtype)
    )
    corrected = (phases - whole_band[None]).astype(jnp.bfloat16)
    return (own, corrected)


def solution(mesh):
    in_specs = (
        P(None, "tile", None),
        P("dir", None, None),
        P("dir", None, None),
        P("tile", "dir", None),
        P("tile", "dir", None, None),
        P("tile", "dir"),
        P("tile", "dir"),
    )
    out_specs = (P("tile", "dir"), P("dir", "tile", None))
    return jax.shard_map(
        on_device, mesh=mesh, in_specs=in_specs, out_specs=out_specs, check_vma=False
    )
```

```python
import jax
import numpy as np
import jax.numpy as jnp
from jax import lax
from jax.experimental import pallas as pl
from jax.experimental.pallas import tpu as pltpu
from jax.sharding import PartitionSpec as P

SPAN = 2
AR_DEV = 3
AC_DEV = 12
ITERS = 3


ridge_weight = 1.0
piston_weight = 0.002
highest = lax.Precision.HIGHEST


def passed_along(array, axis, by):
    size = lax.axis_size(axis)
    return lax.ppermute(array, axis, [(i, (i + by) % size) for i in range(size)])


def band_stack_whole(piece):
    size = lax.axis_size("tile")
    partner = [(i, i ^ 1) for i in range(size)]
    from_below = passed_along(piece, "tile", 2)
    from_above = passed_along(piece, "tile", -2)
    beside = lax.ppermute(piece, "tile", partner)
    second = lax.axis_index("tile") % 2 == 1
    relayed = lax.ppermute(jnp.where(second, from_below, from_above), "tile", partner)
    lower = jnp.where(second, beside, relayed)
    upper = jnp.where(second, relayed, beside)
    return jnp.concatenate([from_below, lower, piece, upper, from_above], axis=1)


def trace_kernel(shift_ref, gain_ref, rim_ref, phase_ref):
    member = pl.program_id(0)
    layers, rim_rows, columns = rim_ref.shape
    band_rows = phase_ref.shape[1]
    rim_depth = (rim_rows - band_rows) // 2
    chunk_rows = band_rows + 16
    total = jnp.zeros((band_rows, columns), jnp.float32)
    row_index = lax.broadcasted_iota(jnp.int32, (band_rows, chunk_rows), 0)
    chunk_index = lax.broadcasted_iota(jnp.int32, (band_rows, chunk_rows), 1)
    for layer_index in range(layers):
        first = rim_depth + shift_ref[member, layer_index, 0]
        start = jnp.clip((first // 16) * 16, 0, rim_rows - chunk_rows)
        start = pl.multiple_of(start, 16)
        lead = first - start
        chunk = rim_ref[layer_index, pl.ds(start, chunk_rows), :].astype(jnp.float32)
        turn = (columns - lax.rem(shift_ref[member, layer_index, 1], columns)) % columns
        window = pltpu.roll(chunk, turn, 1)
        beside = pltpu.roll(window, columns - 1, 1)
        upper = (chunk_index == row_index + lead).astype(jnp.bfloat16)
        lower = (chunk_index == row_index + lead + 1).astype(jnp.bfloat16)
        window = window.astype(jnp.bfloat16)
        beside = beside.astype(jnp.bfloat16)
        top = jnp.dot(upper, window, preferred_element_type=jnp.float32)
        top_beside = jnp.dot(upper, beside, preferred_element_type=jnp.float32)
        bottom = jnp.dot(lower, window, preferred_element_type=jnp.float32)
        bottom_beside = jnp.dot(lower, beside, preferred_element_type=jnp.float32)
        total = total + (
            gain_ref[member, layer_index, 0] * top
            + gain_ref[member, layer_index, 1] * top_beside
            + gain_ref[member, layer_index, 2] * bottom
            + gain_ref[member, layer_index, 3] * bottom_beside
        )
    phase_ref[0] = total


def trace_all(padded_rim, ray_shift, ray_weight, band_rows):
    layers, rim_rows, columns = padded_rim.shape
    members = ray_shift.shape[0]
    return pl.pallas_call(
        trace_kernel,
        out_shape=jax.ShapeDtypeStruct((members, band_rows, columns), jnp.float32),
        grid=(members,),
        in_specs=[
            pl.BlockSpec(memory_space=pltpu.SMEM),
            pl.BlockSpec(memory_space=pltpu.SMEM),
            pl.BlockSpec((layers, rim_rows, columns), lambda m: (0, 0, 0)),
        ],
        out_specs=pl.BlockSpec((1, band_rows, columns), lambda m: (m, 0, 0)),
        compiler_params=pltpu.CompilerParams(vmem_limit_bytes=48 * 1024 * 1024),
    )(ray_shift, ray_weight, padded_rim)


def windows(array, axis, count, stride, width):
    parts = [
        lax.slice_in_dim(array, offset, offset + stride * (count - 1) + 1, stride=stride, axis=axis)
        for offset in range(width)
    ]
    return jnp.stack(parts, axis=axis + 1)


def axis_gather(value, axis, size):
    parts = [value] + [
        lax.ppermute(value, axis, [(i, (i + offset) % size) for i in range(size)])
        for offset in range(1, size)
    ]
    order = (lax.axis_index(axis) - jnp.arange(size)) % size
    return jnp.take(jnp.stack(parts), order, axis=0)


def mesh_gather(value, tile_count, dir_count):
    gathered = axis_gather(axis_gather(value, "dir", dir_count), "tile", tile_count)
    return gathered.reshape((tile_count * dir_count,) + value.shape)


def on_device(screens, ray_shift, ray_weight, influence_index, influence, pupil_mask, petal):
    band_rows = screens.shape[1]
    padded_rim = band_stack_whole(screens)
    arrived = jnp.sum(padded_rim[:, ::band_rows, :1].astype(jnp.float32))
    phases = trace_all(padded_rim, ray_shift, ray_weight, band_rows)
    tile_count = lax.axis_size("tile")
    dir_count = lax.axis_size("dir")
    direction_count = ray_shift.shape[0] * dir_count
    summed = jnp.sum(phases, axis=0)
    block_width = summed.shape[1] // dir_count
    by_block = summed.reshape(band_rows, dir_count, block_width).transpose(1, 0, 2)
    own_column = lax.axis_index("dir")
    column_sum = jnp.take(by_block, own_column, axis=0)
    for offset in range(1, dir_count):
        outgoing = jnp.take(by_block, (own_column + offset) % dir_count, axis=0)
        column_sum = column_sum + lax.ppermute(
            outgoing, "dir", [(i, (i + offset) % dir_count) for i in range(dir_count)]
        )
    mean_phase = column_sum / direction_count
    tiles_here = influence.shape[1]
    near_count = influence.shape[2]
    block_rows, block_columns = petal.shape
    ext_rows, ext_columns = block_rows + 2, block_columns + 2
    extent = ext_rows * ext_columns
    values = influence.astype(jnp.float32)
    onehot = (influence_index[..., None] == jnp.arange(extent, dtype=jnp.int32)).astype(
        jnp.float32
    )
    weights = pupil_mask.astype(jnp.float32).reshape(band_rows, tiles_here, 128)

    masked = (influence * weights[:, :, None, :].astype(jnp.bfloat16))
    gram = jnp.einsum(
        "rckp,rcjp->rckj", masked, influence, preferred_element_type=jnp.float32
    )
    placed = jnp.einsum("rckj,rcjb->rckb", gram, onehot, precision=highest)
    block_matrix = jnp.einsum("rcka,rckb->ab", onehot, placed, precision=highest)

    field = (weights * mean_phase.reshape(band_rows, tiles_here, 128))
    tile_terms = jnp.einsum("rckp,rcp->rck", values, field, precision=highest)
    block_rhs = jnp.einsum("rck,rcka->a", tile_terms, onehot, precision=highest)

    half = extent // 2
    petal_row = jnp.pad(
        petal.reshape(1, -1).astype(jnp.float32), ((0, 0), (0, 3 * half - petal.size))
    )
    early = jnp.concatenate(
        [
            jnp.concatenate(
                [block_matrix[:half, :half], block_matrix[:half, half:], block_matrix[half:, half:]],
                axis=1,
            ),
            petal_row,
        ],
        axis=0,
    )
    block_count = tile_count * dir_count
    early = axis_gather(
        axis_gather(early, "dir", dir_count) + 0.0 * arrived, "tile", tile_count
    ).reshape((block_count,) + early.shape)
    first_part = early[:, :half, :half]
    across_part = early[:, :half, half : 2 * half]
    last_part = early[:, :half, 2 * half :]
    petal_blocks = early[:, half, : petal.size].reshape(
        tile_count, dir_count, block_rows, block_columns
    )
    rhs_blocks = mesh_gather(block_rhs, tile_count, dir_count)
    grid_rows, grid_columns = tile_count * block_rows, dir_count * block_columns
    petal_grid = petal_blocks.transpose(0, 2, 1, 3).reshape(grid_rows, grid_columns)
    active = (petal_grid < 6).astype(jnp.float32)
    petals = (petal_grid[:, :, None] == jnp.arange(6, dtype=jnp.float32)).astype(jnp.float32)

    padded_rows, padded_columns = grid_rows + 2, grid_columns + 2
    row_pick = (
        lax.broadcasted_iota(jnp.int32, (tile_count, ext_rows, padded_rows), 2)
        == block_rows * lax.broadcasted_iota(jnp.int32, (tile_count, ext_rows, padded_rows), 0)
        + lax.broadcasted_iota(jnp.int32, (tile_count, ext_rows, padded_rows), 1)
    ).astype(jnp.float32).reshape(tile_count * ext_rows, padded_rows)
    column_pick = (
        lax.broadcasted_iota(jnp.int32, (padded_columns, dir_count, ext_columns), 0)
        == block_columns
        * lax.broadcasted_iota(jnp.int32, (padded_columns, dir_count, ext_columns), 1)
        + lax.broadcasted_iota(jnp.int32, (padded_columns, dir_count, ext_columns), 2)
    ).astype(jnp.float32).reshape(padded_columns, dir_count * ext_columns)

    def gather_blocks(padded):
        rows = jnp.dot(row_pick, padded, precision=highest)
        picked = jnp.dot(rows, column_pick, precision=highest)
        return (
            picked.reshape(tile_count, ext_rows, dir_count, ext_columns)
            .transpose(0, 2, 1, 3)
            .reshape(block_count, extent)
        )

    def spread_blocks(blocks):
        flat = (
            blocks.reshape(tile_count, dir_count, ext_rows, ext_columns)
            .transpose(0, 2, 1, 3)
            .reshape(tile_count * ext_rows, dir_count * ext_columns)
        )
        rows = jnp.dot(row_pick.T, flat, precision=highest)
        padded = jnp.dot(rows, column_pick.T, precision=highest)
        return padded[1:-1, 1:-1]

    def operator(vector):
        picked = gather_blocks(jnp.pad(vector, 1))
        head, tail = picked[:, :half], picked[:, half:]
        terms = jnp.concatenate(
            [
                jnp.einsum("bij,bj->bi", first_part, head, precision=highest)
                + jnp.einsum("bij,bj->bi", across_part, tail, precision=highest),
                jnp.einsum("bji,bj->bi", across_part, head, precision=highest)
                + jnp.einsum("bij,bj->bi", last_part, tail, precision=highest),
            ],
            axis=1,
        )
        local_part = active * spread_blocks(terms) + ridge_weight * vector
        petal_totals = jnp.einsum("ijp,ij->p", petals, vector, precision=highest)
        return local_part + piston_weight * jnp.einsum(
            "ijp,p->ij", petals, petal_totals, precision=highest
        )

    rhs = active * spread_blocks(rhs_blocks)
    commands = jnp.zeros_like(rhs)
    residual = rhs
    direction = rhs
    norm_now = jnp.sum(residual * residual)
    for step_index in range(ITERS):
        applied = operator(direction)
        step_size = norm_now / jnp.sum(direction * applied)
        commands = commands + step_size * direction
        residual = residual - step_size * applied
        norm_next = jnp.sum(residual * residual)
        direction = residual + (norm_next / norm_now) * direction
        norm_now = norm_next

    row_at = lax.axis_index("tile") * block_rows
    column_at = lax.axis_index("dir") * block_columns
    own = lax.dynamic_slice(commands, (row_at, column_at), (block_rows, block_columns))
    extended = lax.dynamic_slice(
        jnp.pad(commands, 1), (row_at, column_at), (ext_rows, ext_columns)
    )
    picked = jnp.einsum("rcka,a->rck", onehot, extended.reshape(-1), precision=highest)
    fitted = jnp.einsum("rckp,rck->rcp", values, picked, precision=highest).reshape(
        band_rows, tiles_here * 128
    )
    whole_band = (
        axis_gather(fitted.astype(jnp.bfloat16), "dir", dir_count)
        .transpose(1, 0, 2)
        .reshape(band_rows, dir_count * fitted.shape[1])
        .astype(fitted.dtype)
    )
    corrected = (phases - whole_band[None]).astype(jnp.bfloat16)
    return (own, corrected)


def solution(mesh):
    in_specs = (
        P(None, "tile", None),
        P("dir", None, None),
        P("dir", None, None),
        P("tile", "dir", None),
        P("tile", "dir", None, None),
        P("tile", "dir"),
        P("tile", "dir"),
    )
    out_specs = (P("tile", "dir"), P("dir", "tile", None))
    return jax.shard_map(
        on_device, mesh=mesh, in_specs=in_specs, out_specs=out_specs, check_vma=False
    )
```

```python
import jax
import numpy as np
import jax.numpy as jnp
from jax import lax
from jax.experimental import pallas as pl
from jax.experimental.pallas import tpu as pltpu
from jax.sharding import PartitionSpec as P

SPAN = 2
AR_DEV = 3
AC_DEV = 12
ITERS = 3


ridge_weight = 1.0
piston_weight = 0.002
highest = lax.Precision.HIGHEST


def passed_along(array, axis, by):
    size = lax.axis_size(axis)
    return lax.ppermute(array, axis, [(i, (i + by) % size) for i in range(size)])


def band_stack_whole(piece):
    size = lax.axis_size("tile")
    partner = [(i, i ^ 1) for i in range(size)]
    from_below = passed_along(piece, "tile", 2)
    from_above = passed_along(piece, "tile", -2)
    beside = lax.ppermute(piece, "tile", partner)
    second = lax.axis_index("tile") % 2 == 1
    relayed = lax.ppermute(jnp.where(second, from_below, from_above), "tile", partner)
    lower = jnp.where(second, beside, relayed)
    upper = jnp.where(second, relayed, beside)
    return jnp.concatenate([from_below, lower, piece, upper, from_above], axis=1)


def trace_kernel(shift_ref, gain_ref, rim_ref, phase_ref):
    member = pl.program_id(0)
    layers, rim_rows, columns = rim_ref.shape
    band_rows = phase_ref.shape[1]
    rim_depth = (rim_rows - band_rows) // 2
    chunk_rows = band_rows + 16
    total = jnp.zeros((band_rows, columns), jnp.float32)
    row_index = lax.broadcasted_iota(jnp.int32, (band_rows, chunk_rows), 0)
    chunk_index = lax.broadcasted_iota(jnp.int32, (band_rows, chunk_rows), 1)
    for layer_index in range(layers):
        first = rim_depth + shift_ref[member, layer_index, 0]
        start = jnp.clip((first // 16) * 16, 0, rim_rows - chunk_rows)
        start = pl.multiple_of(start, 16)
        lead = first - start
        chunk = rim_ref[layer_index, pl.ds(start, chunk_rows), :]
        column_shift = lax.rem(shift_ref[member, layer_index, 1], columns)
        upper = (chunk_index == row_index + lead).astype(jnp.bfloat16)
        lower = (chunk_index == row_index + lead + 1).astype(jnp.bfloat16)
        top = jnp.dot(upper, chunk, preferred_element_type=jnp.float32)
        bottom = jnp.dot(lower, chunk, preferred_element_type=jnp.float32)
        left = gain_ref[member, layer_index, 0] * top + gain_ref[member, layer_index, 2] * bottom
        right = gain_ref[member, layer_index, 1] * top + gain_ref[member, layer_index, 3] * bottom
        total = total + (
            pltpu.roll(left, (columns - column_shift) % columns, 1)
            + pltpu.roll(right, (2 * columns - column_shift - 1) % columns, 1)
        )
    phase_ref[0] = total


def trace_all(padded_rim, ray_shift, ray_weight, band_rows):
    layers, rim_rows, columns = padded_rim.shape
    members = ray_shift.shape[0]
    return pl.pallas_call(
        trace_kernel,
        out_shape=jax.ShapeDtypeStruct((members, band_rows, columns), jnp.float32),
        grid=(members,),
        in_specs=[
            pl.BlockSpec(memory_space=pltpu.SMEM),
            pl.BlockSpec(memory_space=pltpu.SMEM),
            pl.BlockSpec((layers, rim_rows, columns), lambda m: (0, 0, 0)),
        ],
        out_specs=pl.BlockSpec((1, band_rows, columns), lambda m: (m, 0, 0)),
        compiler_params=pltpu.CompilerParams(vmem_limit_bytes=48 * 1024 * 1024),
    )(ray_shift, ray_weight, padded_rim)


def windows(array, axis, count, stride, width):
    parts = [
        lax.slice_in_dim(array, offset, offset + stride * (count - 1) + 1, stride=stride, axis=axis)
        for offset in range(width)
    ]
    return jnp.stack(parts, axis=axis + 1)


def axis_gather(value, axis, size):
    parts = [value] + [
        lax.ppermute(value, axis, [(i, (i + offset) % size) for i in range(size)])
        for offset in range(1, size)
    ]
    order = (lax.axis_index(axis) - jnp.arange(size)) % size
    return jnp.take(jnp.stack(parts), order, axis=0)


def mesh_gather(value, tile_count, dir_count):
    gathered = axis_gather(axis_gather(value, "dir", dir_count), "tile", tile_count)
    return gathered.reshape((tile_count * dir_count,) + value.shape)


def on_device(screens, ray_shift, ray_weight, influence_index, influence, pupil_mask, petal):
    band_rows = screens.shape[1]
    padded_rim = band_stack_whole(screens)
    arrived = jnp.sum(padded_rim[:, ::band_rows, :1].astype(jnp.float32))
    phases = trace_all(padded_rim, ray_shift, ray_weight, band_rows)
    tile_count = lax.axis_size("tile")
    dir_count = lax.axis_size("dir")
    direction_count = ray_shift.shape[0] * dir_count
    summed = jnp.sum(phases, axis=0)
    block_width = summed.shape[1] // dir_count
    by_block = summed.reshape(band_rows, dir_count, block_width).transpose(1, 0, 2)
    own_column = lax.axis_index("dir")
    column_sum = jnp.take(by_block, own_column, axis=0)
    for offset in range(1, dir_count):
        outgoing = jnp.take(by_block, (own_column + offset) % dir_count, axis=0)
        column_sum = column_sum + lax.ppermute(
            outgoing, "dir", [(i, (i + offset) % dir_count) for i in range(dir_count)]
        )
    mean_phase = column_sum / direction_count
    tiles_here = influence.shape[1]
    near_count = influence.shape[2]
    block_rows, block_columns = petal.shape
    ext_rows, ext_columns = block_rows + 2, block_columns + 2
    extent = ext_rows * ext_columns
    values = influence.astype(jnp.float32)
    onehot = (influence_index[..., None] == jnp.arange(extent, dtype=jnp.int32)).astype(
        jnp.float32
    )
    weights = pupil_mask.astype(jnp.float32).reshape(band_rows, tiles_here, 128)

    masked = (influence * weights[:, :, None, :].astype(jnp.bfloat16))
    gram = jnp.einsum(
        "rckp,rcjp->rckj", masked, influence, preferred_element_type=jnp.float32
    )
    placed = jnp.einsum("rckj,rcjb->rckb", gram, onehot, precision=highest)
    block_matrix = jnp.einsum("rcka,rckb->ab", onehot, placed, precision=highest)

    field = (weights * mean_phase.reshape(band_rows, tiles_here, 128))
    tile_terms = jnp.einsum("rckp,rcp->rck", values, field, precision=highest)
    block_rhs = jnp.einsum("rck,rcka->a", tile_terms, onehot, precision=highest)

    half = extent // 2
    petal_row = jnp.pad(
        petal.reshape(1, -1).astype(jnp.float32), ((0, 0), (0, 3 * half - petal.size))
    )
    early = jnp.concatenate(
        [
            jnp.concatenate(
                [block_matrix[:half, :half], block_matrix[:half, half:], block_matrix[half:, half:]],
                axis=1,
            ),
            petal_row,
        ],
        axis=0,
    )
    block_count = tile_count * dir_count
    early = axis_gather(
        axis_gather(early, "dir", dir_count) + 0.0 * arrived, "tile", tile_count
    ).reshape((block_count,) + early.shape)
    first_part = early[:, :half, :half]
    across_part = early[:, :half, half : 2 * half]
    last_part = early[:, :half, 2 * half :]
    petal_blocks = early[:, half, : petal.size].reshape(
        tile_count, dir_count, block_rows, block_columns
    )
    rhs_blocks = mesh_gather(block_rhs, tile_count, dir_count)
    grid_rows, grid_columns = tile_count * block_rows, dir_count * block_columns
    petal_grid = petal_blocks.transpose(0, 2, 1, 3).reshape(grid_rows, grid_columns)
    active = (petal_grid < 6).astype(jnp.float32)
    petals = (petal_grid[:, :, None] == jnp.arange(6, dtype=jnp.float32)).astype(jnp.float32)

    padded_rows, padded_columns = grid_rows + 2, grid_columns + 2
    row_pick = (
        lax.broadcasted_iota(jnp.int32, (tile_count, ext_rows, padded_rows), 2)
        == block_rows * lax.broadcasted_iota(jnp.int32, (tile_count, ext_rows, padded_rows), 0)
        + lax.broadcasted_iota(jnp.int32, (tile_count, ext_rows, padded_rows), 1)
    ).astype(jnp.float32).reshape(tile_count * ext_rows, padded_rows)
    column_pick = (
        lax.broadcasted_iota(jnp.int32, (padded_columns, dir_count, ext_columns), 0)
        == block_columns
        * lax.broadcasted_iota(jnp.int32, (padded_columns, dir_count, ext_columns), 1)
        + lax.broadcasted_iota(jnp.int32, (padded_columns, dir_count, ext_columns), 2)
    ).astype(jnp.float32).reshape(padded_columns, dir_count * ext_columns)

    def gather_blocks(padded):
        rows = jnp.dot(row_pick, padded, precision=highest)
        picked = jnp.dot(rows, column_pick, precision=highest)
        return (
            picked.reshape(tile_count, ext_rows, dir_count, ext_columns)
            .transpose(0, 2, 1, 3)
            .reshape(block_count, extent)
        )

    def spread_blocks(blocks):
        flat = (
            blocks.reshape(tile_count, dir_count, ext_rows, ext_columns)
            .transpose(0, 2, 1, 3)
            .reshape(tile_count * ext_rows, dir_count * ext_columns)
        )
        rows = jnp.dot(row_pick.T, flat, precision=highest)
        padded = jnp.dot(rows, column_pick.T, precision=highest)
        return padded[1:-1, 1:-1]

    def operator(vector):
        picked = gather_blocks(jnp.pad(vector, 1))
        head, tail = picked[:, :half], picked[:, half:]
        terms = jnp.concatenate(
            [
                jnp.einsum("bij,bj->bi", first_part, head, precision=highest)
                + jnp.einsum("bij,bj->bi", across_part, tail, precision=highest),
                jnp.einsum("bji,bj->bi", across_part, head, precision=highest)
                + jnp.einsum("bij,bj->bi", last_part, tail, precision=highest),
            ],
            axis=1,
        )
        local_part = active * spread_blocks(terms) + ridge_weight * vector
        petal_totals = jnp.einsum("ijp,ij->p", petals, vector, precision=highest)
        return local_part + piston_weight * jnp.einsum(
            "ijp,p->ij", petals, petal_totals, precision=highest
        )

    rhs = active * spread_blocks(rhs_blocks)
    commands = jnp.zeros_like(rhs)
    residual = rhs
    direction = rhs
    norm_now = jnp.sum(residual * residual)
    for step_index in range(ITERS):
        applied = operator(direction)
        step_size = norm_now / jnp.sum(direction * applied)
        commands = commands + step_size * direction
        residual = residual - step_size * applied
        norm_next = jnp.sum(residual * residual)
        direction = residual + (norm_next / norm_now) * direction
        norm_now = norm_next

    row_at = lax.axis_index("tile") * block_rows
    column_at = lax.axis_index("dir") * block_columns
    own = lax.dynamic_slice(commands, (row_at, column_at), (block_rows, block_columns))
    extended = lax.dynamic_slice(
        jnp.pad(commands, 1), (row_at, column_at), (ext_rows, ext_columns)
    )
    picked = jnp.einsum("rcka,a->rck", onehot, extended.reshape(-1), precision=highest)
    fitted = jnp.einsum("rckp,rck->rcp", values, picked, precision=highest).reshape(
        band_rows, tiles_here * 128
    )
    whole_band = (
        axis_gather(fitted.astype(jnp.bfloat16), "dir", dir_count)
        .transpose(1, 0, 2)
        .reshape(band_rows, dir_count * fitted.shape[1])
        .astype(fitted.dtype)
    )
    corrected = (phases - whole_band[None]).astype(jnp.bfloat16)
    return (own, corrected)


def solution(mesh):
    in_specs = (
        P(None, "tile", None),
        P("dir", None, None),
        P("dir", None, None),
        P("tile", "dir", None),
        P("tile", "dir", None, None),
        P("tile", "dir"),
        P("tile", "dir"),
    )
    out_specs = (P("tile", "dir"), P("dir", "tile", None))
    return jax.shard_map(
        on_device, mesh=mesh, in_specs=in_specs, out_specs=out_specs, check_vma=False
    )
```

```python
import jax
import numpy as np
import jax.numpy as jnp
from jax import lax
from jax.experimental import pallas as pl
from jax.experimental.pallas import tpu as pltpu
from jax.sharding import PartitionSpec as P

SPAN = 2
AR_DEV = 3
AC_DEV = 12
ITERS = 3


ridge_weight = 1.0
piston_weight = 0.002
highest = lax.Precision.HIGHEST


def passed_along(array, axis, by):
    size = lax.axis_size(axis)
    return lax.ppermute(array, axis, [(i, (i + by) % size) for i in range(size)])


def band_stack_whole(piece):
    size = lax.axis_size("tile")
    partner = [(i, i ^ 1) for i in range(size)]
    from_below = passed_along(piece, "tile", 2)
    from_above = passed_along(piece, "tile", -2)
    beside = lax.ppermute(piece, "tile", partner)
    second = lax.axis_index("tile") % 2 == 1
    relayed_below = lax.ppermute(from_below, "tile", partner)
    relayed_above = lax.ppermute(from_above, "tile", partner)
    lower = jnp.where(second, beside, relayed_below)
    upper = jnp.where(second, relayed_above, beside)
    return jnp.concatenate([from_below, lower, piece, upper, from_above], axis=1)


def trace_kernel(shift_ref, gain_ref, rim_ref, phase_ref):
    member = pl.program_id(0)
    layers, rim_rows, columns = rim_ref.shape
    band_rows = phase_ref.shape[1]
    rim_depth = (rim_rows - band_rows) // 2
    chunk_rows = band_rows + 16
    total = jnp.zeros((band_rows, columns), jnp.float32)
    row_index = lax.broadcasted_iota(jnp.int32, (band_rows, chunk_rows), 0)
    chunk_index = lax.broadcasted_iota(jnp.int32, (band_rows, chunk_rows), 1)
    for layer_index in range(layers):
        first = rim_depth + shift_ref[member, layer_index, 0]
        start = jnp.clip((first // 16) * 16, 0, rim_rows - chunk_rows)
        start = pl.multiple_of(start, 16)
        lead = first - start
        chunk = rim_ref[layer_index, pl.ds(start, chunk_rows), :]
        column_shift = lax.rem(shift_ref[member, layer_index, 1], columns)
        upper = (chunk_index == row_index + lead).astype(jnp.bfloat16)
        lower = (chunk_index == row_index + lead + 1).astype(jnp.bfloat16)
        top = jnp.dot(upper, chunk, preferred_element_type=jnp.float32)
        bottom = jnp.dot(lower, chunk, preferred_element_type=jnp.float32)
        left = gain_ref[member, layer_index, 0] * top + gain_ref[member, layer_index, 2] * bottom
        right = gain_ref[member, layer_index, 1] * top + gain_ref[member, layer_index, 3] * bottom
        total = total + (
            pltpu.roll(left, (columns - column_shift) % columns, 1)
            + pltpu.roll(right, (2 * columns - column_shift - 1) % columns, 1)
        )
    phase_ref[0] = total


def trace_all(padded_rim, ray_shift, ray_weight, band_rows):
    layers, rim_rows, columns = padded_rim.shape
    members = ray_shift.shape[0]
    return pl.pallas_call(
        trace_kernel,
        out_shape=jax.ShapeDtypeStruct((members, band_rows, columns), jnp.float32),
        grid=(members,),
        in_specs=[
            pl.BlockSpec(memory_space=pltpu.SMEM),
            pl.BlockSpec(memory_space=pltpu.SMEM),
            pl.BlockSpec((layers, rim_rows, columns), lambda m: (0, 0, 0)),
        ],
        out_specs=pl.BlockSpec((1, band_rows, columns), lambda m: (m, 0, 0)),
        compiler_params=pltpu.CompilerParams(vmem_limit_bytes=48 * 1024 * 1024),
    )(ray_shift, ray_weight, padded_rim)


def windows(array, axis, count, stride, width):
    parts = [
        lax.slice_in_dim(array, offset, offset + stride * (count - 1) + 1, stride=stride, axis=axis)
        for offset in range(width)
    ]
    return jnp.stack(parts, axis=axis + 1)


def axis_gather(value, axis, size):
    parts = [value] + [
        lax.ppermute(value, axis, [(i, (i + offset) % size) for i in range(size)])
        for offset in range(1, size)
    ]
    order = (lax.axis_index(axis) - jnp.arange(size)) % size
    return jnp.take(jnp.stack(parts), order, axis=0)


def mesh_gather(value, tile_count, dir_count):
    gathered = axis_gather(axis_gather(value, "dir", dir_count), "tile", tile_count)
    return gathered.reshape((tile_count * dir_count,) + value.shape)


def on_device(screens, ray_shift, ray_weight, influence_index, influence, pupil_mask, petal):
    band_rows = screens.shape[1]
    padded_rim = band_stack_whole(screens)
    arrived = jnp.sum(padded_rim[:, ::band_rows, :1].astype(jnp.float32))
    phases = trace_all(padded_rim, ray_shift, ray_weight, band_rows)
    tile_count = lax.axis_size("tile")
    dir_count = lax.axis_size("dir")
    direction_count = ray_shift.shape[0] * dir_count
    summed = jnp.sum(phases, axis=0)
    block_width = summed.shape[1] // dir_count
    by_block = summed.reshape(band_rows, dir_count, block_width).transpose(1, 0, 2)
    own_column = lax.axis_index("dir")
    column_sum = jnp.take(by_block, own_column, axis=0)
    for offset in range(1, dir_count):
        outgoing = jnp.take(by_block, (own_column + offset) % dir_count, axis=0)
        column_sum = column_sum + lax.ppermute(
            outgoing, "dir", [(i, (i + offset) % dir_count) for i in range(dir_count)]
        )
    mean_phase = column_sum / direction_count
    tiles_here = influence.shape[1]
    near_count = influence.shape[2]
    block_rows, block_columns = petal.shape
    ext_rows, ext_columns = block_rows + 2, block_columns + 2
    extent = ext_rows * ext_columns
    values = influence.astype(jnp.float32)
    onehot = (influence_index[..., None] == jnp.arange(extent, dtype=jnp.int32)).astype(
        jnp.float32
    )
    weights = pupil_mask.astype(jnp.float32).reshape(band_rows, tiles_here, 128)

    masked = (influence * weights[:, :, None, :].astype(jnp.bfloat16))
    gram = jnp.einsum(
        "rckp,rcjp->rckj", masked, influence, preferred_element_type=jnp.float32
    )
    placed = jnp.einsum("rckj,rcjb->rckb", gram, onehot, precision=highest)
    block_matrix = jnp.einsum("rcka,rckb->ab", onehot, placed, precision=highest)

    field = (weights * mean_phase.reshape(band_rows, tiles_here, 128))
    tile_terms = jnp.einsum("rckp,rcp->rck", values, field, precision=highest)
    block_rhs = jnp.einsum("rck,rcka->a", tile_terms, onehot, precision=highest)

    half = extent // 2
    petal_row = jnp.pad(
        petal.reshape(1, -1).astype(jnp.float32), ((0, 0), (0, 3 * half - petal.size))
    )
    early = jnp.concatenate(
        [
            jnp.concatenate(
                [block_matrix[:half, :half], block_matrix[:half, half:], block_matrix[half:, half:]],
                axis=1,
            ),
            petal_row,
        ],
        axis=0,
    )
    block_count = tile_count * dir_count
    early = axis_gather(
        axis_gather(early, "dir", dir_count) + 0.0 * arrived, "tile", tile_count
    ).reshape((block_count,) + early.shape)
    first_part = early[:, :half, :half]
    across_part = early[:, :half, half : 2 * half]
    last_part = early[:, :half, 2 * half :]
    petal_blocks = early[:, half, : petal.size].reshape(
        tile_count, dir_count, block_rows, block_columns
    )
    rhs_blocks = mesh_gather(block_rhs, tile_count, dir_count)
    grid_rows, grid_columns = tile_count * block_rows, dir_count * block_columns
    petal_grid = petal_blocks.transpose(0, 2, 1, 3).reshape(grid_rows, grid_columns)
    active = (petal_grid < 6).astype(jnp.float32)
    petals = (petal_grid[:, :, None] == jnp.arange(6, dtype=jnp.float32)).astype(jnp.float32)

    padded_rows, padded_columns = grid_rows + 2, grid_columns + 2
    row_pick = (
        lax.broadcasted_iota(jnp.int32, (tile_count, ext_rows, padded_rows), 2)
        == block_rows * lax.broadcasted_iota(jnp.int32, (tile_count, ext_rows, padded_rows), 0)
        + lax.broadcasted_iota(jnp.int32, (tile_count, ext_rows, padded_rows), 1)
    ).astype(jnp.float32).reshape(tile_count * ext_rows, padded_rows)
    column_pick = (
        lax.broadcasted_iota(jnp.int32, (padded_columns, dir_count, ext_columns), 0)
        == block_columns
        * lax.broadcasted_iota(jnp.int32, (padded_columns, dir_count, ext_columns), 1)
        + lax.broadcasted_iota(jnp.int32, (padded_columns, dir_count, ext_columns), 2)
    ).astype(jnp.float32).reshape(padded_columns, dir_count * ext_columns)

    def gather_blocks(padded):
        rows = jnp.dot(row_pick, padded, precision=highest)
        picked = jnp.dot(rows, column_pick, precision=highest)
        return (
            picked.reshape(tile_count, ext_rows, dir_count, ext_columns)
            .transpose(0, 2, 1, 3)
            .reshape(block_count, extent)
        )

    def spread_blocks(blocks):
        flat = (
            blocks.reshape(tile_count, dir_count, ext_rows, ext_columns)
            .transpose(0, 2, 1, 3)
            .reshape(tile_count * ext_rows, dir_count * ext_columns)
        )
        rows = jnp.dot(row_pick.T, flat, precision=highest)
        padded = jnp.dot(rows, column_pick.T, precision=highest)
        return padded[1:-1, 1:-1]

    def operator(vector):
        picked = gather_blocks(jnp.pad(vector, 1))
        head, tail = picked[:, :half], picked[:, half:]
        terms = jnp.concatenate(
            [
                jnp.einsum("bij,bj->bi", first_part, head, precision=highest)
                + jnp.einsum("bij,bj->bi", across_part, tail, precision=highest),
                jnp.einsum("bji,bj->bi", across_part, head, precision=highest)
                + jnp.einsum("bij,bj->bi", last_part, tail, precision=highest),
            ],
            axis=1,
        )
        local_part = active * spread_blocks(terms) + ridge_weight * vector
        petal_totals = jnp.einsum("ijp,ij->p", petals, vector, precision=highest)
        return local_part + piston_weight * jnp.einsum(
            "ijp,p->ij", petals, petal_totals, precision=highest
        )

    rhs = active * spread_blocks(rhs_blocks)
    commands = jnp.zeros_like(rhs)
    residual = rhs
    direction = rhs
    norm_now = jnp.sum(residual * residual)
    for step_index in range(ITERS):
        applied = operator(direction)
        step_size = norm_now / jnp.sum(direction * applied)
        commands = commands + step_size * direction
        residual = residual - step_size * applied
        norm_next = jnp.sum(residual * residual)
        direction = residual + (norm_next / norm_now) * direction
        norm_now = norm_next

    row_at = lax.axis_index("tile") * block_rows
    column_at = lax.axis_index("dir") * block_columns
    own = lax.dynamic_slice(commands, (row_at, column_at), (block_rows, block_columns))
    extended = lax.dynamic_slice(
        jnp.pad(commands, 1), (row_at, column_at), (ext_rows, ext_columns)
    )
    picked = jnp.einsum("rcka,a->rck", onehot, extended.reshape(-1), precision=highest)
    fitted = jnp.einsum("rckp,rck->rcp", values, picked, precision=highest).reshape(
        band_rows, tiles_here * 128
    )
    whole_band = (
        axis_gather(fitted.astype(jnp.bfloat16), "dir", dir_count)
        .transpose(1, 0, 2)
        .reshape(band_rows, dir_count * fitted.shape[1])
        .astype(fitted.dtype)
    )
    corrected = (phases - whole_band[None]).astype(jnp.bfloat16)
    return (own, corrected)


def solution(mesh):
    in_specs = (
        P(None, "tile", None),
        P("dir", None, None),
        P("dir", None, None),
        P("tile", "dir", None),
        P("tile", "dir", None, None),
        P("tile", "dir"),
        P("tile", "dir"),
    )
    out_specs = (P("tile", "dir"), P("dir", "tile", None))
    return jax.shard_map(
        on_device, mesh=mesh, in_specs=in_specs, out_specs=out_specs, check_vma=False
    )
```

```python
import jax
import numpy as np
import jax.numpy as jnp
from jax import lax
from jax.experimental import pallas as pl
from jax.experimental.pallas import tpu as pltpu
from jax.sharding import PartitionSpec as P

SPAN = 2
AR_DEV = 3
AC_DEV = 12
ITERS = 3


ridge_weight = 1.0
piston_weight = 0.002
highest = lax.Precision.HIGHEST


def passed_along(array, axis, by):
    size = lax.axis_size(axis)
    return lax.ppermute(array, axis, [(i, (i + by) % size) for i in range(size)])


def band_stack_whole(piece):
    size = lax.axis_size("tile")
    partner = [(i, i ^ 1) for i in range(size)]
    from_below = passed_along(piece, "tile", 2)
    from_above = passed_along(piece, "tile", -2)
    beside = lax.ppermute(piece, "tile", partner)
    second = lax.axis_index("tile") % 2 == 1
    relayed_below = lax.ppermute(from_below, "tile", partner)
    relayed_above = lax.ppermute(from_above, "tile", partner)
    lower = jnp.where(second, beside, relayed_below)
    upper = jnp.where(second, relayed_above, beside)
    return [from_below, lower, piece, upper, from_above]


def trace_kernel(shift_ref, gain_ref, *refs):
    band_refs, phase_ref, chunk_ref = refs[:-2], refs[-2], refs[-1]
    member = pl.program_id(0)
    layers, band_rows, columns = band_refs[0].shape
    chunk_rows = band_rows + 16
    rim_rows = band_rows * len(band_refs)
    rim_depth = (rim_rows - band_rows) // 2
    total = jnp.zeros((band_rows, columns), jnp.float32)
    row_index = lax.broadcasted_iota(jnp.int32, (band_rows, chunk_rows), 0)
    chunk_index = lax.broadcasted_iota(jnp.int32, (band_rows, chunk_rows), 1)
    for layer_index in range(layers):
        first = rim_depth + shift_ref[member, layer_index, 0]
        start = jnp.clip((first // 16) * 16, 0, rim_rows - chunk_rows)
        lead = first - start
        band_at = start // band_rows
        inside = start % band_rows
        for band in range(len(band_refs) - 1):
            for offset in range(0, band_rows, 16):

                @pl.when((band_at == band) & (inside == offset))
                def _():
                    chunk_ref[: band_rows - offset, :] = band_refs[band][layer_index, offset:, :]
                    chunk_ref[band_rows - offset :, :] = band_refs[band + 1][
                        layer_index, : offset + 16, :
                    ]

        chunk = chunk_ref[...]
        column_shift = lax.rem(shift_ref[member, layer_index, 1], columns)
        upper = (chunk_index == row_index + lead).astype(jnp.bfloat16)
        lower = (chunk_index == row_index + lead + 1).astype(jnp.bfloat16)
        top = jnp.dot(upper, chunk, preferred_element_type=jnp.float32)
        bottom = jnp.dot(lower, chunk, preferred_element_type=jnp.float32)
        left = gain_ref[member, layer_index, 0] * top + gain_ref[member, layer_index, 2] * bottom
        right = gain_ref[member, layer_index, 1] * top + gain_ref[member, layer_index, 3] * bottom
        total = total + (
            pltpu.roll(left, (columns - column_shift) % columns, 1)
            + pltpu.roll(right, (2 * columns - column_shift - 1) % columns, 1)
        )
    phase_ref[0] = total


def trace_all(bands, ray_shift, ray_weight, band_rows):
    layers, _, columns = bands[0].shape
    members = ray_shift.shape[0]
    band_spec = pl.BlockSpec((layers, band_rows, columns), lambda m: (0, 0, 0))
    return pl.pallas_call(
        trace_kernel,
        out_shape=jax.ShapeDtypeStruct((members, band_rows, columns), jnp.float32),
        grid=(members,),
        in_specs=[pl.BlockSpec(memory_space=pltpu.SMEM), pl.BlockSpec(memory_space=pltpu.SMEM)]
        + [band_spec] * len(bands),
        out_specs=pl.BlockSpec((1, band_rows, columns), lambda m: (m, 0, 0)),
        scratch_shapes=[pltpu.VMEM((band_rows + 16, columns), bands[0].dtype)],
        compiler_params=pltpu.CompilerParams(vmem_limit_bytes=48 * 1024 * 1024),
    )(ray_shift, ray_weight, *bands)


def windows(array, axis, count, stride, width):
    parts = [
        lax.slice_in_dim(array, offset, offset + stride * (count - 1) + 1, stride=stride, axis=axis)
        for offset in range(width)
    ]
    return jnp.stack(parts, axis=axis + 1)


def axis_gather(value, axis, size):
    parts = [value] + [
        lax.ppermute(value, axis, [(i, (i + offset) % size) for i in range(size)])
        for offset in range(1, size)
    ]
    order = (lax.axis_index(axis) - jnp.arange(size)) % size
    return jnp.take(jnp.stack(parts), order, axis=0)


def mesh_gather(value, tile_count, dir_count):
    gathered = axis_gather(axis_gather(value, "dir", dir_count), "tile", tile_count)
    return gathered.reshape((tile_count * dir_count,) + value.shape)


def on_device(screens, ray_shift, ray_weight, influence_index, influence, pupil_mask, petal):
    band_rows = screens.shape[1]
    padded_rim = band_stack_whole(screens)
    arrived = sum(jnp.sum(band[:, :1, :1].astype(jnp.float32)) for band in padded_rim)
    phases = trace_all(padded_rim, ray_shift, ray_weight, band_rows)
    tile_count = lax.axis_size("tile")
    dir_count = lax.axis_size("dir")
    direction_count = ray_shift.shape[0] * dir_count
    summed = jnp.sum(phases, axis=0)
    block_width = summed.shape[1] // dir_count
    by_block = summed.reshape(band_rows, dir_count, block_width).transpose(1, 0, 2)
    own_column = lax.axis_index("dir")
    column_sum = jnp.take(by_block, own_column, axis=0)
    for offset in range(1, dir_count):
        outgoing = jnp.take(by_block, (own_column + offset) % dir_count, axis=0)
        column_sum = column_sum + lax.ppermute(
            outgoing, "dir", [(i, (i + offset) % dir_count) for i in range(dir_count)]
        )
    mean_phase = column_sum / direction_count
    tiles_here = influence.shape[1]
    near_count = influence.shape[2]
    block_rows, block_columns = petal.shape
    ext_rows, ext_columns = block_rows + 2, block_columns + 2
    extent = ext_rows * ext_columns
    values = influence.astype(jnp.float32)
    onehot = (influence_index[..., None] == jnp.arange(extent, dtype=jnp.int32)).astype(
        jnp.float32
    )
    weights = pupil_mask.astype(jnp.float32).reshape(band_rows, tiles_here, 128)

    masked = (influence * weights[:, :, None, :].astype(jnp.bfloat16))
    gram = jnp.einsum(
        "rckp,rcjp->rckj", masked, influence, preferred_element_type=jnp.float32
    )
    placed = jnp.einsum("rckj,rcjb->rckb", gram, onehot, precision=highest)
    block_matrix = jnp.einsum("rcka,rckb->ab", onehot, placed, precision=highest)

    field = (weights * mean_phase.reshape(band_rows, tiles_here, 128))
    tile_terms = jnp.einsum("rckp,rcp->rck", values, field, precision=highest)
    block_rhs = jnp.einsum("rck,rcka->a", tile_terms, onehot, precision=highest)

    half = extent // 2
    petal_row = jnp.pad(
        petal.reshape(1, -1).astype(jnp.float32), ((0, 0), (0, 3 * half - petal.size))
    )
    early = jnp.concatenate(
        [
            jnp.concatenate(
                [block_matrix[:half, :half], block_matrix[:half, half:], block_matrix[half:, half:]],
                axis=1,
            ),
            petal_row,
        ],
        axis=0,
    )
    block_count = tile_count * dir_count
    early = axis_gather(
        axis_gather(early, "dir", dir_count) + 0.0 * arrived, "tile", tile_count
    ).reshape((block_count,) + early.shape)
    first_part = early[:, :half, :half]
    across_part = early[:, :half, half : 2 * half]
    last_part = early[:, :half, 2 * half :]
    petal_blocks = early[:, half, : petal.size].reshape(
        tile_count, dir_count, block_rows, block_columns
    )
    rhs_blocks = mesh_gather(block_rhs, tile_count, dir_count)
    grid_rows, grid_columns = tile_count * block_rows, dir_count * block_columns
    petal_grid = petal_blocks.transpose(0, 2, 1, 3).reshape(grid_rows, grid_columns)
    active = (petal_grid < 6).astype(jnp.float32)
    petals = (petal_grid[:, :, None] == jnp.arange(6, dtype=jnp.float32)).astype(jnp.float32)

    padded_rows, padded_columns = grid_rows + 2, grid_columns + 2
    row_pick = (
        lax.broadcasted_iota(jnp.int32, (tile_count, ext_rows, padded_rows), 2)
        == block_rows * lax.broadcasted_iota(jnp.int32, (tile_count, ext_rows, padded_rows), 0)
        + lax.broadcasted_iota(jnp.int32, (tile_count, ext_rows, padded_rows), 1)
    ).astype(jnp.float32).reshape(tile_count * ext_rows, padded_rows)
    column_pick = (
        lax.broadcasted_iota(jnp.int32, (padded_columns, dir_count, ext_columns), 0)
        == block_columns
        * lax.broadcasted_iota(jnp.int32, (padded_columns, dir_count, ext_columns), 1)
        + lax.broadcasted_iota(jnp.int32, (padded_columns, dir_count, ext_columns), 2)
    ).astype(jnp.float32).reshape(padded_columns, dir_count * ext_columns)

    def gather_blocks(padded):
        rows = jnp.dot(row_pick, padded, precision=highest)
        picked = jnp.dot(rows, column_pick, precision=highest)
        return (
            picked.reshape(tile_count, ext_rows, dir_count, ext_columns)
            .transpose(0, 2, 1, 3)
            .reshape(block_count, extent)
        )

    def spread_blocks(blocks):
        flat = (
            blocks.reshape(tile_count, dir_count, ext_rows, ext_columns)
            .transpose(0, 2, 1, 3)
            .reshape(tile_count * ext_rows, dir_count * ext_columns)
        )
        rows = jnp.dot(row_pick.T, flat, precision=highest)
        padded = jnp.dot(rows, column_pick.T, precision=highest)
        return padded[1:-1, 1:-1]

    def operator(vector):
        picked = gather_blocks(jnp.pad(vector, 1))
        head, tail = picked[:, :half], picked[:, half:]
        terms = jnp.concatenate(
            [
                jnp.einsum("bij,bj->bi", first_part, head, precision=highest)
                + jnp.einsum("bij,bj->bi", across_part, tail, precision=highest),
                jnp.einsum("bji,bj->bi", across_part, head, precision=highest)
                + jnp.einsum("bij,bj->bi", last_part, tail, precision=highest),
            ],
            axis=1,
        )
        local_part = active * spread_blocks(terms) + ridge_weight * vector
        petal_totals = jnp.einsum("ijp,ij->p", petals, vector, precision=highest)
        return local_part + piston_weight * jnp.einsum(
            "ijp,p->ij", petals, petal_totals, precision=highest
        )

    rhs = active * spread_blocks(rhs_blocks)
    commands = jnp.zeros_like(rhs)
    residual = rhs
    direction = rhs
    norm_now = jnp.sum(residual * residual)
    for step_index in range(ITERS):
        applied = operator(direction)
        step_size = norm_now / jnp.sum(direction * applied)
        commands = commands + step_size * direction
        residual = residual - step_size * applied
        norm_next = jnp.sum(residual * residual)
        direction = residual + (norm_next / norm_now) * direction
        norm_now = norm_next

    row_at = lax.axis_index("tile") * block_rows
    column_at = lax.axis_index("dir") * block_columns
    own = lax.dynamic_slice(commands, (row_at, column_at), (block_rows, block_columns))
    extended = lax.dynamic_slice(
        jnp.pad(commands, 1), (row_at, column_at), (ext_rows, ext_columns)
    )
    picked = jnp.einsum("rcka,a->rck", onehot, extended.reshape(-1), precision=highest)
    fitted = jnp.einsum("rckp,rck->rcp", values, picked, precision=highest).reshape(
        band_rows, tiles_here * 128
    )
    whole_band = (
        axis_gather(fitted.astype(jnp.bfloat16), "dir", dir_count)
        .transpose(1, 0, 2)
        .reshape(band_rows, dir_count * fitted.shape[1])
        .astype(fitted.dtype)
    )
    corrected = (phases - whole_band[None]).astype(jnp.bfloat16)
    return (own, corrected)


def solution(mesh):
    in_specs = (
        P(None, "tile", None),
        P("dir", None, None),
        P("dir", None, None),
        P("tile", "dir", None),
        P("tile", "dir", None, None),
        P("tile", "dir"),
        P("tile", "dir"),
    )
    out_specs = (P("tile", "dir"), P("dir", "tile", None))
    return jax.shard_map(
        on_device, mesh=mesh, in_specs=in_specs, out_specs=out_specs, check_vma=False
    )
```

```python
import jax
import numpy as np
import jax.numpy as jnp
from jax import lax
from jax.experimental import pallas as pl
from jax.experimental.pallas import tpu as pltpu
from jax.sharding import PartitionSpec as P

SPAN = 2
AR_DEV = 3
AC_DEV = 12
ITERS = 3


ridge_weight = 1.0
piston_weight = 0.002
highest = lax.Precision.HIGHEST


def passed_along(array, axis, by):
    size = lax.axis_size(axis)
    return lax.ppermute(array, axis, [(i, (i + by) % size) for i in range(size)])


def band_stack_whole(piece):
    size = lax.axis_size("tile")
    partner = [(i, i ^ 1) for i in range(size)]
    from_below = passed_along(piece, "tile", 2)
    from_above = passed_along(piece, "tile", -2)
    beside = lax.ppermute(piece, "tile", partner)
    second = lax.axis_index("tile") % 2 == 1
    relayed = lax.ppermute(jnp.where(second, from_below, from_above), "tile", partner)
    lower = jnp.where(second, beside, relayed)
    upper = jnp.where(second, relayed, beside)
    return jnp.concatenate([from_below, lower, piece, upper, from_above], axis=1)


def trace_kernel(shift_ref, gain_ref, rim_ref, phase_ref):
    layer_index = pl.program_id(0)
    _, rim_rows, columns = rim_ref.shape
    members, band_rows, _ = phase_ref.shape
    rim_depth = (rim_rows - band_rows) // 2
    chunk_rows = band_rows + 16
    row_index = lax.broadcasted_iota(jnp.int32, (band_rows, chunk_rows), 0)
    chunk_index = lax.broadcasted_iota(jnp.int32, (band_rows, chunk_rows), 1)

    @pl.when(layer_index == 0)
    def _():
        phase_ref[...] = jnp.zeros(phase_ref.shape, phase_ref.dtype)

    for member in range(members):
        first = rim_depth + shift_ref[member, layer_index, 0]
        start = jnp.clip((first // 16) * 16, 0, rim_rows - chunk_rows)
        start = pl.multiple_of(start, 16)
        lead = first - start
        chunk = rim_ref[0, pl.ds(start, chunk_rows), :]
        column_shift = lax.rem(shift_ref[member, layer_index, 1], columns)
        upper = (chunk_index == row_index + lead).astype(jnp.bfloat16)
        lower = (chunk_index == row_index + lead + 1).astype(jnp.bfloat16)
        top = jnp.dot(upper, chunk, preferred_element_type=jnp.float32)
        bottom = jnp.dot(lower, chunk, preferred_element_type=jnp.float32)
        left = gain_ref[member, layer_index, 0] * top + gain_ref[member, layer_index, 2] * bottom
        right = gain_ref[member, layer_index, 1] * top + gain_ref[member, layer_index, 3] * bottom
        phase_ref[member] = phase_ref[member] + (
            pltpu.roll(left, (columns - column_shift) % columns, 1)
            + pltpu.roll(right, (2 * columns - column_shift - 1) % columns, 1)
        )


def trace_all(padded_rim, ray_shift, ray_weight, band_rows):
    layers, rim_rows, columns = padded_rim.shape
    members = ray_shift.shape[0]
    return pl.pallas_call(
        trace_kernel,
        out_shape=jax.ShapeDtypeStruct((members, band_rows, columns), jnp.float32),
        grid=(layers,),
        in_specs=[
            pl.BlockSpec(memory_space=pltpu.SMEM),
            pl.BlockSpec(memory_space=pltpu.SMEM),
            pl.BlockSpec((1, rim_rows, columns), lambda layer: (layer, 0, 0)),
        ],
        out_specs=pl.BlockSpec((members, band_rows, columns), lambda layer: (0, 0, 0)),
        compiler_params=pltpu.CompilerParams(vmem_limit_bytes=48 * 1024 * 1024),
    )(ray_shift, ray_weight, padded_rim)


def windows(array, axis, count, stride, width):
    parts = [
        lax.slice_in_dim(array, offset, offset + stride * (count - 1) + 1, stride=stride, axis=axis)
        for offset in range(width)
    ]
    return jnp.stack(parts, axis=axis + 1)


def axis_gather(value, axis, size):
    parts = [value] + [
        lax.ppermute(value, axis, [(i, (i + offset) % size) for i in range(size)])
        for offset in range(1, size)
    ]
    order = (lax.axis_index(axis) - jnp.arange(size)) % size
    return jnp.take(jnp.stack(parts), order, axis=0)


def mesh_gather(value, tile_count, dir_count):
    gathered = axis_gather(axis_gather(value, "dir", dir_count), "tile", tile_count)
    return gathered.reshape((tile_count * dir_count,) + value.shape)


def on_device(screens, ray_shift, ray_weight, influence_index, influence, pupil_mask, petal):
    band_rows = screens.shape[1]
    padded_rim = band_stack_whole(screens)
    arrived = jnp.sum(padded_rim[:, ::band_rows, :1].astype(jnp.float32))
    phases = trace_all(padded_rim, ray_shift, ray_weight, band_rows)
    tile_count = lax.axis_size("tile")
    dir_count = lax.axis_size("dir")
    direction_count = ray_shift.shape[0] * dir_count
    summed = jnp.sum(phases, axis=0)
    block_width = summed.shape[1] // dir_count
    by_block = summed.reshape(band_rows, dir_count, block_width).transpose(1, 0, 2)
    own_column = lax.axis_index("dir")
    column_sum = jnp.take(by_block, own_column, axis=0)
    for offset in range(1, dir_count):
        outgoing = jnp.take(by_block, (own_column + offset) % dir_count, axis=0)
        column_sum = column_sum + lax.ppermute(
            outgoing, "dir", [(i, (i + offset) % dir_count) for i in range(dir_count)]
        )
    mean_phase = column_sum / direction_count
    tiles_here = influence.shape[1]
    near_count = influence.shape[2]
    block_rows, block_columns = petal.shape
    ext_rows, ext_columns = block_rows + 2, block_columns + 2
    extent = ext_rows * ext_columns
    values = influence.astype(jnp.float32)
    onehot = (influence_index[..., None] == jnp.arange(extent, dtype=jnp.int32)).astype(
        jnp.float32
    )
    weights = pupil_mask.astype(jnp.float32).reshape(band_rows, tiles_here, 128)

    masked = (influence * weights[:, :, None, :].astype(jnp.bfloat16))
    gram = jnp.einsum(
        "rckp,rcjp->rckj", masked, influence, preferred_element_type=jnp.float32
    )
    placed = jnp.einsum("rckj,rcjb->rckb", gram, onehot, precision=highest)
    block_matrix = jnp.einsum("rcka,rckb->ab", onehot, placed, precision=highest)

    field = (weights * mean_phase.reshape(band_rows, tiles_here, 128))
    tile_terms = jnp.einsum("rckp,rcp->rck", values, field, precision=highest)
    block_rhs = jnp.einsum("rck,rcka->a", tile_terms, onehot, precision=highest)

    half = extent // 2
    petal_row = jnp.pad(
        petal.reshape(1, -1).astype(jnp.float32), ((0, 0), (0, 3 * half - petal.size))
    )
    early = jnp.concatenate(
        [
            jnp.concatenate(
                [block_matrix[:half, :half], block_matrix[:half, half:], block_matrix[half:, half:]],
                axis=1,
            ),
            petal_row,
        ],
        axis=0,
    )
    block_count = tile_count * dir_count
    early = axis_gather(
        axis_gather(early, "dir", dir_count) + 0.0 * arrived, "tile", tile_count
    ).reshape((block_count,) + early.shape)
    first_part = early[:, :half, :half]
    across_part = early[:, :half, half : 2 * half]
    last_part = early[:, :half, 2 * half :]
    petal_blocks = early[:, half, : petal.size].reshape(
        tile_count, dir_count, block_rows, block_columns
    )
    rhs_blocks = mesh_gather(block_rhs, tile_count, dir_count)
    grid_rows, grid_columns = tile_count * block_rows, dir_count * block_columns
    petal_grid = petal_blocks.transpose(0, 2, 1, 3).reshape(grid_rows, grid_columns)
    active = (petal_grid < 6).astype(jnp.float32)
    petals = (petal_grid[:, :, None] == jnp.arange(6, dtype=jnp.float32)).astype(jnp.float32)

    padded_rows, padded_columns = grid_rows + 2, grid_columns + 2
    row_pick = (
        lax.broadcasted_iota(jnp.int32, (tile_count, ext_rows, padded_rows), 2)
        == block_rows * lax.broadcasted_iota(jnp.int32, (tile_count, ext_rows, padded_rows), 0)
        + lax.broadcasted_iota(jnp.int32, (tile_count, ext_rows, padded_rows), 1)
    ).astype(jnp.float32).reshape(tile_count * ext_rows, padded_rows)
    column_pick = (
        lax.broadcasted_iota(jnp.int32, (padded_columns, dir_count, ext_columns), 0)
        == block_columns
        * lax.broadcasted_iota(jnp.int32, (padded_columns, dir_count, ext_columns), 1)
        + lax.broadcasted_iota(jnp.int32, (padded_columns, dir_count, ext_columns), 2)
    ).astype(jnp.float32).reshape(padded_columns, dir_count * ext_columns)

    def gather_blocks(padded):
        rows = jnp.dot(row_pick, padded, precision=highest)
        picked = jnp.dot(rows, column_pick, precision=highest)
        return (
            picked.reshape(tile_count, ext_rows, dir_count, ext_columns)
            .transpose(0, 2, 1, 3)
            .reshape(block_count, extent)
        )

    def spread_blocks(blocks):
        flat = (
            blocks.reshape(tile_count, dir_count, ext_rows, ext_columns)
            .transpose(0, 2, 1, 3)
            .reshape(tile_count * ext_rows, dir_count * ext_columns)
        )
        rows = jnp.dot(row_pick.T, flat, precision=highest)
        padded = jnp.dot(rows, column_pick.T, precision=highest)
        return padded[1:-1, 1:-1]

    def operator(vector):
        picked = gather_blocks(jnp.pad(vector, 1))
        head, tail = picked[:, :half], picked[:, half:]
        terms = jnp.concatenate(
            [
                jnp.einsum("bij,bj->bi", first_part, head, precision=highest)
                + jnp.einsum("bij,bj->bi", across_part, tail, precision=highest),
                jnp.einsum("bji,bj->bi", across_part, head, precision=highest)
                + jnp.einsum("bij,bj->bi", last_part, tail, precision=highest),
            ],
            axis=1,
        )
        local_part = active * spread_blocks(terms) + ridge_weight * vector
        petal_totals = jnp.einsum("ijp,ij->p", petals, vector, precision=highest)
        return local_part + piston_weight * jnp.einsum(
            "ijp,p->ij", petals, petal_totals, precision=highest
        )

    rhs = active * spread_blocks(rhs_blocks)
    commands = jnp.zeros_like(rhs)
    residual = rhs
    direction = rhs
    norm_now = jnp.sum(residual * residual)
    for step_index in range(ITERS):
        applied = operator(direction)
        step_size = norm_now / jnp.sum(direction * applied)
        commands = commands + step_size * direction
        residual = residual - step_size * applied
        norm_next = jnp.sum(residual * residual)
        direction = residual + (norm_next / norm_now) * direction
        norm_now = norm_next

    row_at = lax.axis_index("tile") * block_rows
    column_at = lax.axis_index("dir") * block_columns
    own = lax.dynamic_slice(commands, (row_at, column_at), (block_rows, block_columns))
    extended = lax.dynamic_slice(
        jnp.pad(commands, 1), (row_at, column_at), (ext_rows, ext_columns)
    )
    picked = jnp.einsum("rcka,a->rck", onehot, extended.reshape(-1), precision=highest)
    fitted = jnp.einsum("rckp,rck->rcp", values, picked, precision=highest).reshape(
        band_rows, tiles_here * 128
    )
    whole_band = (
        axis_gather(fitted.astype(jnp.bfloat16), "dir", dir_count)
        .transpose(1, 0, 2)
        .reshape(band_rows, dir_count * fitted.shape[1])
        .astype(fitted.dtype)
    )
    corrected = (phases - whole_band[None]).astype(jnp.bfloat16)
    return (own, corrected)


def solution(mesh):
    in_specs = (
        P(None, "tile", None),
        P("dir", None, None),
        P("dir", None, None),
        P("tile", "dir", None),
        P("tile", "dir", None, None),
        P("tile", "dir"),
        P("tile", "dir"),
    )
    out_specs = (P("tile", "dir"), P("dir", "tile", None))
    return jax.shard_map(
        on_device, mesh=mesh, in_specs=in_specs, out_specs=out_specs, check_vma=False
    )
```

```python
import jax
import numpy as np
import jax.numpy as jnp
from jax import lax
from jax.experimental import pallas as pl
from jax.experimental.pallas import tpu as pltpu
from jax.sharding import PartitionSpec as P

SPAN = 2
AR_DEV = 3
AC_DEV = 12
ITERS = 3


ridge_weight = 1.0
piston_weight = 0.002
highest = lax.Precision.HIGHEST


def passed_along(array, axis, by):
    size = lax.axis_size(axis)
    return lax.ppermute(array, axis, [(i, (i + by) % size) for i in range(size)])


def band_stack_whole(piece):
    size = lax.axis_size("tile")
    partner = [(i, i ^ 1) for i in range(size)]
    from_below = passed_along(piece, "tile", 2)
    from_above = passed_along(piece, "tile", -2)
    beside = lax.ppermute(piece, "tile", partner)
    second = lax.axis_index("tile") % 2 == 1
    relayed = lax.ppermute(jnp.where(second, from_below, from_above), "tile", partner)
    lower = jnp.where(second, beside, relayed)
    upper = jnp.where(second, relayed, beside)
    return jnp.concatenate([from_below, lower, piece, upper, from_above], axis=1)


def trace_kernel(shift_ref, gain_ref, rim_ref, phase_ref, sum_ref):
    layer_index = pl.program_id(0)
    _, rim_rows, columns = rim_ref.shape
    members, band_rows, _ = phase_ref.shape
    rim_depth = (rim_rows - band_rows) // 2
    chunk_rows = band_rows + 16
    row_index = lax.broadcasted_iota(jnp.int32, (band_rows, chunk_rows), 0)
    chunk_index = lax.broadcasted_iota(jnp.int32, (band_rows, chunk_rows), 1)

    @pl.when(layer_index == 0)
    def _():
        phase_ref[...] = jnp.zeros(phase_ref.shape, phase_ref.dtype)

    for member in range(members):
        first = rim_depth + shift_ref[member, layer_index, 0]
        start = jnp.clip((first // 16) * 16, 0, rim_rows - chunk_rows)
        start = pl.multiple_of(start, 16)
        lead = first - start
        chunk = rim_ref[0, pl.ds(start, chunk_rows), :]
        column_shift = lax.rem(shift_ref[member, layer_index, 1], columns)
        upper = (chunk_index == row_index + lead).astype(jnp.bfloat16)
        lower = (chunk_index == row_index + lead + 1).astype(jnp.bfloat16)
        top = jnp.dot(upper, chunk, preferred_element_type=jnp.float32)
        bottom = jnp.dot(lower, chunk, preferred_element_type=jnp.float32)
        left = gain_ref[member, layer_index, 0] * top + gain_ref[member, layer_index, 2] * bottom
        right = gain_ref[member, layer_index, 1] * top + gain_ref[member, layer_index, 3] * bottom
        phase_ref[member] = phase_ref[member] + (
            pltpu.roll(left, (columns - column_shift) % columns, 1)
            + pltpu.roll(right, (2 * columns - column_shift - 1) % columns, 1)
        )

    @pl.when(layer_index == pl.num_programs(0) - 1)
    def _():
        across = phase_ref[0]
        for member in range(1, members):
            across = across + phase_ref[member]
        sum_ref[...] = across


def trace_all(padded_rim, ray_shift, ray_weight, band_rows):
    layers, rim_rows, columns = padded_rim.shape
    members = ray_shift.shape[0]
    return pl.pallas_call(
        trace_kernel,
        out_shape=(
            jax.ShapeDtypeStruct((members, band_rows, columns), jnp.float32),
            jax.ShapeDtypeStruct((band_rows, columns), jnp.float32),
        ),
        grid=(layers,),
        in_specs=[
            pl.BlockSpec(memory_space=pltpu.SMEM),
            pl.BlockSpec(memory_space=pltpu.SMEM),
            pl.BlockSpec((1, rim_rows, columns), lambda layer: (layer, 0, 0)),
        ],
        out_specs=(
            pl.BlockSpec((members, band_rows, columns), lambda layer: (0, 0, 0)),
            pl.BlockSpec((band_rows, columns), lambda layer: (0, 0)),
        ),
        compiler_params=pltpu.CompilerParams(vmem_limit_bytes=48 * 1024 * 1024),
    )(ray_shift, ray_weight, padded_rim)


def windows(array, axis, count, stride, width):
    parts = [
        lax.slice_in_dim(array, offset, offset + stride * (count - 1) + 1, stride=stride, axis=axis)
        for offset in range(width)
    ]
    return jnp.stack(parts, axis=axis + 1)


def axis_gather(value, axis, size):
    parts = [value] + [
        lax.ppermute(value, axis, [(i, (i + offset) % size) for i in range(size)])
        for offset in range(1, size)
    ]
    order = (lax.axis_index(axis) - jnp.arange(size)) % size
    return jnp.take(jnp.stack(parts), order, axis=0)


def mesh_gather(value, tile_count, dir_count):
    gathered = axis_gather(axis_gather(value, "dir", dir_count), "tile", tile_count)
    return gathered.reshape((tile_count * dir_count,) + value.shape)


def on_device(screens, ray_shift, ray_weight, influence_index, influence, pupil_mask, petal):
    band_rows = screens.shape[1]
    padded_rim = band_stack_whole(screens)
    arrived = jnp.sum(padded_rim[:, ::band_rows, :1].astype(jnp.float32))
    phases, summed = trace_all(padded_rim, ray_shift, ray_weight, band_rows)
    tile_count = lax.axis_size("tile")
    dir_count = lax.axis_size("dir")
    direction_count = ray_shift.shape[0] * dir_count
    block_width = summed.shape[1] // dir_count
    by_block = summed.reshape(band_rows, dir_count, block_width).transpose(1, 0, 2)
    own_column = lax.axis_index("dir")
    column_sum = jnp.take(by_block, own_column, axis=0)
    for offset in range(1, dir_count):
        outgoing = jnp.take(by_block, (own_column + offset) % dir_count, axis=0)
        column_sum = column_sum + lax.ppermute(
            outgoing, "dir", [(i, (i + offset) % dir_count) for i in range(dir_count)]
        )
    mean_phase = column_sum / direction_count
    tiles_here = influence.shape[1]
    near_count = influence.shape[2]
    block_rows, block_columns = petal.shape
    ext_rows, ext_columns = block_rows + 2, block_columns + 2
    extent = ext_rows * ext_columns
    values = influence.astype(jnp.float32)
    onehot = (influence_index[..., None] == jnp.arange(extent, dtype=jnp.int32)).astype(
        jnp.float32
    )
    weights = pupil_mask.astype(jnp.float32).reshape(band_rows, tiles_here, 128)

    masked = (influence * weights[:, :, None, :].astype(jnp.bfloat16))
    gram = jnp.einsum(
        "rckp,rcjp->rckj", masked, influence, preferred_element_type=jnp.float32
    )
    placed = jnp.einsum("rckj,rcjb->rckb", gram, onehot, precision=highest)
    block_matrix = jnp.einsum("rcka,rckb->ab", onehot, placed, precision=highest)

    field = (weights * mean_phase.reshape(band_rows, tiles_here, 128))
    tile_terms = jnp.einsum("rckp,rcp->rck", values, field, precision=highest)
    block_rhs = jnp.einsum("rck,rcka->a", tile_terms, onehot, precision=highest)

    half = extent // 2
    petal_row = jnp.pad(
        petal.reshape(1, -1).astype(jnp.float32), ((0, 0), (0, 3 * half - petal.size))
    )
    early = jnp.concatenate(
        [
            jnp.concatenate(
                [block_matrix[:half, :half], block_matrix[:half, half:], block_matrix[half:, half:]],
                axis=1,
            ),
            petal_row,
        ],
        axis=0,
    )
    block_count = tile_count * dir_count
    early = axis_gather(
        axis_gather(early, "dir", dir_count) + 0.0 * arrived, "tile", tile_count
    ).reshape((block_count,) + early.shape)
    first_part = early[:, :half, :half]
    across_part = early[:, :half, half : 2 * half]
    last_part = early[:, :half, 2 * half :]
    petal_blocks = early[:, half, : petal.size].reshape(
        tile_count, dir_count, block_rows, block_columns
    )
    rhs_blocks = mesh_gather(block_rhs, tile_count, dir_count)
    grid_rows, grid_columns = tile_count * block_rows, dir_count * block_columns
    petal_grid = petal_blocks.transpose(0, 2, 1, 3).reshape(grid_rows, grid_columns)
    active = (petal_grid < 6).astype(jnp.float32)
    petals = (petal_grid[:, :, None] == jnp.arange(6, dtype=jnp.float32)).astype(jnp.float32)

    padded_rows, padded_columns = grid_rows + 2, grid_columns + 2
    row_pick = (
        lax.broadcasted_iota(jnp.int32, (tile_count, ext_rows, padded_rows), 2)
        == block_rows * lax.broadcasted_iota(jnp.int32, (tile_count, ext_rows, padded_rows), 0)
        + lax.broadcasted_iota(jnp.int32, (tile_count, ext_rows, padded_rows), 1)
    ).astype(jnp.float32).reshape(tile_count * ext_rows, padded_rows)
    column_pick = (
        lax.broadcasted_iota(jnp.int32, (padded_columns, dir_count, ext_columns), 0)
        == block_columns
        * lax.broadcasted_iota(jnp.int32, (padded_columns, dir_count, ext_columns), 1)
        + lax.broadcasted_iota(jnp.int32, (padded_columns, dir_count, ext_columns), 2)
    ).astype(jnp.float32).reshape(padded_columns, dir_count * ext_columns)

    def gather_blocks(padded):
        rows = jnp.dot(row_pick, padded, precision=highest)
        picked = jnp.dot(rows, column_pick, precision=highest)
        return (
            picked.reshape(tile_count, ext_rows, dir_count, ext_columns)
            .transpose(0, 2, 1, 3)
            .reshape(block_count, extent)
        )

    def spread_blocks(blocks):
        flat = (
            blocks.reshape(tile_count, dir_count, ext_rows, ext_columns)
            .transpose(0, 2, 1, 3)
            .reshape(tile_count * ext_rows, dir_count * ext_columns)
        )
        rows = jnp.dot(row_pick.T, flat, precision=highest)
        padded = jnp.dot(rows, column_pick.T, precision=highest)
        return padded[1:-1, 1:-1]

    def operator(vector):
        picked = gather_blocks(jnp.pad(vector, 1))
        head, tail = picked[:, :half], picked[:, half:]
        terms = jnp.concatenate(
            [
                jnp.einsum("bij,bj->bi", first_part, head, precision=highest)
                + jnp.einsum("bij,bj->bi", across_part, tail, precision=highest),
                jnp.einsum("bji,bj->bi", across_part, head, precision=highest)
                + jnp.einsum("bij,bj->bi", last_part, tail, precision=highest),
            ],
            axis=1,
        )
        local_part = active * spread_blocks(terms) + ridge_weight * vector
        petal_totals = jnp.einsum("ijp,ij->p", petals, vector, precision=highest)
        return local_part + piston_weight * jnp.einsum(
            "ijp,p->ij", petals, petal_totals, precision=highest
        )

    rhs = active * spread_blocks(rhs_blocks)
    commands = jnp.zeros_like(rhs)
    residual = rhs
    direction = rhs
    norm_now = jnp.sum(residual * residual)
    for step_index in range(ITERS):
        applied = operator(direction)
        step_size = norm_now / jnp.sum(direction * applied)
        commands = commands + step_size * direction
        residual = residual - step_size * applied
        norm_next = jnp.sum(residual * residual)
        direction = residual + (norm_next / norm_now) * direction
        norm_now = norm_next

    row_at = lax.axis_index("tile") * block_rows
    column_at = lax.axis_index("dir") * block_columns
    own = lax.dynamic_slice(commands, (row_at, column_at), (block_rows, block_columns))
    extended = lax.dynamic_slice(
        jnp.pad(commands, 1), (row_at, column_at), (ext_rows, ext_columns)
    )
    picked = jnp.einsum("rcka,a->rck", onehot, extended.reshape(-1), precision=highest)
    fitted = jnp.einsum("rckp,rck->rcp", values, picked, precision=highest).reshape(
        band_rows, tiles_here * 128
    )
    whole_band = (
        axis_gather(fitted.astype(jnp.bfloat16), "dir", dir_count)
        .transpose(1, 0, 2)
        .reshape(band_rows, dir_count * fitted.shape[1])
        .astype(fitted.dtype)
    )
    corrected = (phases - whole_band[None]).astype(jnp.bfloat16)
    return (own, corrected)


def solution(mesh):
    in_specs = (
        P(None, "tile", None),
        P("dir", None, None),
        P("dir", None, None),
        P("tile", "dir", None),
        P("tile", "dir", None, None),
        P("tile", "dir"),
        P("tile", "dir"),
    )
    out_specs = (P("tile", "dir"), P("dir", "tile", None))
    return jax.shard_map(
        on_device, mesh=mesh, in_specs=in_specs, out_specs=out_specs, check_vma=False
    )
```

```python
import jax
import numpy as np
import jax.numpy as jnp
from jax import lax
from jax.experimental import pallas as pl
from jax.experimental.pallas import tpu as pltpu
from jax.sharding import PartitionSpec as P

SPAN = 2
AR_DEV = 3
AC_DEV = 12
ITERS = 3


ridge_weight = 1.0
piston_weight = 0.002
highest = lax.Precision.HIGHEST


def passed_along(array, axis, by):
    size = lax.axis_size(axis)
    return lax.ppermute(array, axis, [(i, (i + by) % size) for i in range(size)])


def band_stack_whole(piece):
    size = lax.axis_size("tile")
    partner = [(i, i ^ 1) for i in range(size)]
    from_below = passed_along(piece, "tile", 2)
    from_above = passed_along(piece, "tile", -2)
    beside = lax.ppermute(piece, "tile", partner)
    second = lax.axis_index("tile") % 2 == 1
    relayed_below = lax.ppermute(from_below, "tile", partner)
    relayed_above = lax.ppermute(from_above, "tile", partner)
    lower = jnp.where(second, beside, relayed_below)
    upper = jnp.where(second, relayed_above, beside)
    return jnp.concatenate([from_below, lower, piece, upper, from_above], axis=1)


def trace_kernel(shift_ref, gain_ref, rim_ref, phase_ref, sum_ref):
    layer_index = pl.program_id(0)
    _, rim_rows, columns = rim_ref.shape
    members, band_rows, _ = phase_ref.shape
    rim_depth = (rim_rows - band_rows) // 2
    chunk_rows = band_rows + 16
    row_index = lax.broadcasted_iota(jnp.int32, (band_rows, chunk_rows), 0)
    chunk_index = lax.broadcasted_iota(jnp.int32, (band_rows, chunk_rows), 1)

    @pl.when(layer_index == 0)
    def _():
        phase_ref[...] = jnp.zeros(phase_ref.shape, phase_ref.dtype)

    for member in range(members):
        first = rim_depth + shift_ref[member, layer_index, 0]
        start = jnp.clip((first // 16) * 16, 0, rim_rows - chunk_rows)
        start = pl.multiple_of(start, 16)
        lead = first - start
        chunk = rim_ref[0, pl.ds(start, chunk_rows), :]
        column_shift = lax.rem(shift_ref[member, layer_index, 1], columns)
        upper = (chunk_index == row_index + lead).astype(jnp.bfloat16)
        lower = (chunk_index == row_index + lead + 1).astype(jnp.bfloat16)
        top = jnp.dot(upper, chunk, preferred_element_type=jnp.float32)
        bottom = jnp.dot(lower, chunk, preferred_element_type=jnp.float32)
        left = gain_ref[member, layer_index, 0] * top + gain_ref[member, layer_index, 2] * bottom
        right = gain_ref[member, layer_index, 1] * top + gain_ref[member, layer_index, 3] * bottom
        phase_ref[member] = phase_ref[member] + (
            pltpu.roll(left, (columns - column_shift) % columns, 1)
            + pltpu.roll(right, (2 * columns - column_shift - 1) % columns, 1)
        )

    @pl.when(layer_index == pl.num_programs(0) - 1)
    def _():
        across = phase_ref[0]
        for member in range(1, members):
            across = across + phase_ref[member]
        sum_ref[...] = across


def trace_all(padded_rim, ray_shift, ray_weight, band_rows):
    layers, rim_rows, columns = padded_rim.shape
    members = ray_shift.shape[0]
    return pl.pallas_call(
        trace_kernel,
        out_shape=(
            jax.ShapeDtypeStruct((members, band_rows, columns), jnp.float32),
            jax.ShapeDtypeStruct((band_rows, columns), jnp.float32),
        ),
        grid=(layers,),
        in_specs=[
            pl.BlockSpec(memory_space=pltpu.SMEM),
            pl.BlockSpec(memory_space=pltpu.SMEM),
            pl.BlockSpec((1, rim_rows, columns), lambda layer: (layer, 0, 0)),
        ],
        out_specs=(
            pl.BlockSpec((members, band_rows, columns), lambda layer: (0, 0, 0)),
            pl.BlockSpec((band_rows, columns), lambda layer: (0, 0)),
        ),
        compiler_params=pltpu.CompilerParams(vmem_limit_bytes=48 * 1024 * 1024),
    )(ray_shift, ray_weight, padded_rim)


def windows(array, axis, count, stride, width):
    parts = [
        lax.slice_in_dim(array, offset, offset + stride * (count - 1) + 1, stride=stride, axis=axis)
        for offset in range(width)
    ]
    return jnp.stack(parts, axis=axis + 1)


def axis_gather(value, axis, size):
    parts = [value] + [
        lax.ppermute(value, axis, [(i, (i + offset) % size) for i in range(size)])
        for offset in range(1, size)
    ]
    order = (lax.axis_index(axis) - jnp.arange(size)) % size
    return jnp.take(jnp.stack(parts), order, axis=0)


def mesh_gather(value, tile_count, dir_count):
    gathered = axis_gather(axis_gather(value, "dir", dir_count), "tile", tile_count)
    return gathered.reshape((tile_count * dir_count,) + value.shape)


def on_device(screens, ray_shift, ray_weight, influence_index, influence, pupil_mask, petal):
    band_rows = screens.shape[1]
    padded_rim = band_stack_whole(screens)
    arrived = jnp.sum(padded_rim[:, ::band_rows, :1].astype(jnp.float32))
    phases, summed = trace_all(padded_rim, ray_shift, ray_weight, band_rows)
    tile_count = lax.axis_size("tile")
    dir_count = lax.axis_size("dir")
    direction_count = ray_shift.shape[0] * dir_count
    block_width = summed.shape[1] // dir_count
    by_block = summed.reshape(band_rows, dir_count, block_width).transpose(1, 0, 2)
    own_column = lax.axis_index("dir")
    column_sum = jnp.take(by_block, own_column, axis=0)
    for offset in range(1, dir_count):
        outgoing = jnp.take(by_block, (own_column + offset) % dir_count, axis=0)
        column_sum = column_sum + lax.ppermute(
            outgoing, "dir", [(i, (i + offset) % dir_count) for i in range(dir_count)]
        )
    mean_phase = column_sum / direction_count
    tiles_here = influence.shape[1]
    near_count = influence.shape[2]
    block_rows, block_columns = petal.shape
    ext_rows, ext_columns = block_rows + 2, block_columns + 2
    extent = ext_rows * ext_columns
    values = influence.astype(jnp.float32)
    onehot = (influence_index[..., None] == jnp.arange(extent, dtype=jnp.int32)).astype(
        jnp.float32
    )
    weights = pupil_mask.astype(jnp.float32).reshape(band_rows, tiles_here, 128)

    masked = (influence * weights[:, :, None, :].astype(jnp.bfloat16))
    gram = jnp.einsum(
        "rckp,rcjp->rckj", masked, influence, preferred_element_type=jnp.float32
    )
    placed = jnp.einsum("rckj,rcjb->rckb", gram, onehot, precision=highest)
    block_matrix = jnp.einsum("rcka,rckb->ab", onehot, placed, precision=highest)

    field = (weights * mean_phase.reshape(band_rows, tiles_here, 128))
    tile_terms = jnp.einsum("rckp,rcp->rck", values, field, precision=highest)
    block_rhs = jnp.einsum("rck,rcka->a", tile_terms, onehot, precision=highest)

    half = extent // 2
    petal_row = jnp.pad(
        petal.reshape(1, -1).astype(jnp.float32), ((0, 0), (0, 3 * half - petal.size))
    )
    early = jnp.concatenate(
        [
            jnp.concatenate(
                [block_matrix[:half, :half], block_matrix[:half, half:], block_matrix[half:, half:]],
                axis=1,
            ),
            petal_row,
        ],
        axis=0,
    )
    block_count = tile_count * dir_count
    early = axis_gather(
        axis_gather(early, "dir", dir_count) + 0.0 * arrived, "tile", tile_count
    ).reshape((block_count,) + early.shape)
    first_part = early[:, :half, :half]
    across_part = early[:, :half, half : 2 * half]
    last_part = early[:, :half, 2 * half :]
    petal_blocks = early[:, half, : petal.size].reshape(
        tile_count, dir_count, block_rows, block_columns
    )
    rhs_blocks = mesh_gather(block_rhs, tile_count, dir_count)
    grid_rows, grid_columns = tile_count * block_rows, dir_count * block_columns
    petal_grid = petal_blocks.transpose(0, 2, 1, 3).reshape(grid_rows, grid_columns)
    active = (petal_grid < 6).astype(jnp.float32)
    petals = (petal_grid[:, :, None] == jnp.arange(6, dtype=jnp.float32)).astype(jnp.float32)

    padded_rows, padded_columns = grid_rows + 2, grid_columns + 2
    row_pick = (
        lax.broadcasted_iota(jnp.int32, (tile_count, ext_rows, padded_rows), 2)
        == block_rows * lax.broadcasted_iota(jnp.int32, (tile_count, ext_rows, padded_rows), 0)
        + lax.broadcasted_iota(jnp.int32, (tile_count, ext_rows, padded_rows), 1)
    ).astype(jnp.float32).reshape(tile_count * ext_rows, padded_rows)
    column_pick = (
        lax.broadcasted_iota(jnp.int32, (padded_columns, dir_count, ext_columns), 0)
        == block_columns
        * lax.broadcasted_iota(jnp.int32, (padded_columns, dir_count, ext_columns), 1)
        + lax.broadcasted_iota(jnp.int32, (padded_columns, dir_count, ext_columns), 2)
    ).astype(jnp.float32).reshape(padded_columns, dir_count * ext_columns)

    def gather_blocks(padded):
        rows = jnp.dot(row_pick, padded, precision=highest)
        picked = jnp.dot(rows, column_pick, precision=highest)
        return (
            picked.reshape(tile_count, ext_rows, dir_count, ext_columns)
            .transpose(0, 2, 1, 3)
            .reshape(block_count, extent)
        )

    def spread_blocks(blocks):
        flat = (
            blocks.reshape(tile_count, dir_count, ext_rows, ext_columns)
            .transpose(0, 2, 1, 3)
            .reshape(tile_count * ext_rows, dir_count * ext_columns)
        )
        rows = jnp.dot(row_pick.T, flat, precision=highest)
        padded = jnp.dot(rows, column_pick.T, precision=highest)
        return padded[1:-1, 1:-1]

    def operator(vector):
        picked = gather_blocks(jnp.pad(vector, 1))
        head, tail = picked[:, :half], picked[:, half:]
        terms = jnp.concatenate(
            [
                jnp.einsum("bij,bj->bi", first_part, head, precision=highest)
                + jnp.einsum("bij,bj->bi", across_part, tail, precision=highest),
                jnp.einsum("bji,bj->bi", across_part, head, precision=highest)
                + jnp.einsum("bij,bj->bi", last_part, tail, precision=highest),
            ],
            axis=1,
        )
        local_part = active * spread_blocks(terms) + ridge_weight * vector
        petal_totals = jnp.einsum("ijp,ij->p", petals, vector, precision=highest)
        return local_part + piston_weight * jnp.einsum(
            "ijp,p->ij", petals, petal_totals, precision=highest
        )

    rhs = active * spread_blocks(rhs_blocks)
    commands = jnp.zeros_like(rhs)
    residual = rhs
    direction = rhs
    norm_now = jnp.sum(residual * residual)
    for step_index in range(ITERS):
        applied = operator(direction)
        step_size = norm_now / jnp.sum(direction * applied)
        commands = commands + step_size * direction
        residual = residual - step_size * applied
        norm_next = jnp.sum(residual * residual)
        direction = residual + (norm_next / norm_now) * direction
        norm_now = norm_next

    row_at = lax.axis_index("tile") * block_rows
    column_at = lax.axis_index("dir") * block_columns
    own = lax.dynamic_slice(commands, (row_at, column_at), (block_rows, block_columns))
    extended = lax.dynamic_slice(
        jnp.pad(commands, 1), (row_at, column_at), (ext_rows, ext_columns)
    )
    picked = jnp.einsum("rcka,a->rck", onehot, extended.reshape(-1), precision=highest)
    fitted = jnp.einsum("rckp,rck->rcp", values, picked, precision=highest).reshape(
        band_rows, tiles_here * 128
    )
    whole_band = (
        axis_gather(fitted.astype(jnp.bfloat16), "dir", dir_count)
        .transpose(1, 0, 2)
        .reshape(band_rows, dir_count * fitted.shape[1])
        .astype(fitted.dtype)
    )
    corrected = (phases - whole_band[None]).astype(jnp.bfloat16)
    return (own, corrected)


def solution(mesh):
    in_specs = (
        P(None, "tile", None),
        P("dir", None, None),
        P("dir", None, None),
        P("tile", "dir", None),
        P("tile", "dir", None, None),
        P("tile", "dir"),
        P("tile", "dir"),
    )
    out_specs = (P("tile", "dir"), P("dir", "tile", None))
    return jax.shard_map(
        on_device, mesh=mesh, in_specs=in_specs, out_specs=out_specs, check_vma=False
    )
```
